128 devices in a mesh: dof: 32 (over x, z, core), snap: 4 (over y).
Axes of the slice: x: 4, y: 4, z: 4, core: 2. Of those that a mesh axis runs over, the one named last changes fastest.
Arguments:
- snapshots: bfloat16 [131072, 1024], P('dof', 'snap')
- lengths: int32 [16], replicated, may hold values from 16 to 64, as said below
- start_block: float32 [1024, 128], replicated, may hold values from -6 to 6
Outputs:
- pod_modes: float32 [131072, 128], P(('dof', 'snap'))
- r_factor: float32 [1024, 1024], replicated
The draws below stay inside these ranges and needn't reach their ends.
Inputs may be any that keep to these rules, and one draw needn't show every extreme that they name: `lengths`: some passage has all 64 steps active and some passage only a quarter of them.
All inputs are finite; a program needn't handle non-finite values.
Results may differ from the reference program's by a relative error of at most 0.0003.
Values may be sent and summed in bfloat16 or wider, within the bound.
No kernel may reach another device: no remote copies, remote signals or barrier semaphores. Data moves between devices by JAX's collectives and lax.ppermute only.
A program may use at most 128 MiB of HBM per device.

```python
import math
import jax
import jax.numpy as jnp
from jax import lax

NS = 1024
STEPS = 64
MODES = 128
ITERS = 3
PASSES = 16
M = 131072


def draw_snapshots(key, part):
    keys = jax.random.split(key, 3)
    row_scale = jnp.exp(jax.random.uniform(keys[0], (M, 1), jnp.float32, math.log(0.3), math.log(3.0)))
    col_scale = jnp.exp(jax.random.uniform(keys[1], (1, NS), jnp.float32, math.log(0.3), math.log(3.0)))
    base = jax.random.normal(keys[2], (M, NS), jnp.float32)
    return (base * row_scale * col_scale).astype(jnp.bfloat16)


def draw_lengths(key, part):
    keys = jax.random.split(key, 2)
    values = jax.random.randint(keys[0], (PASSES,), STEPS // 4, STEPS + 1)
    order = jax.random.permutation(keys[1], PASSES)
    values = values.at[order[0]].set(STEPS)
    values = values.at[order[1]].set(STEPS // 4)
    return values.astype(jnp.int32)


def centred(rng, extent, scale, most, kind=jnp.bfloat16):
    return jnp.clip(scale * jax.random.normal(rng, extent, jnp.float32), -most, most).astype(kind)


def setup_inputs(seed: int = 0) -> dict:
    splits = jax.random.split(jax.random.key(seed), 4)
    return {
        "snapshots": draw_snapshots(jax.random.fold_in(splits[3], 71), 0),
        "lengths": draw_lengths(jax.random.fold_in(splits[3], 71), 0),
        "start_block": centred(splits[2], (NS, MODES), 1.0, 6.0, jnp.float32),
    }


def reference(snapshots, lengths, start_block):
    columns = jnp.arange(NS, dtype=jnp.int32)
    col_length = lengths[(columns // STEPS).astype(jnp.int32)]
    active = columns % STEPS < col_length
    masked = jnp.where(active[None, :], snapshots, jnp.zeros_like(snapshots))
    gram_sum = jnp.dot(masked.T.astype(jnp.float32), masked.astype(jnp.float32), preferred_element_type=jnp.float32)
    shifted = gram_sum / jnp.float32(M) + 0.05 * jnp.eye(NS, dtype=jnp.float32)
    upper_factor = jnp.linalg.cholesky(shifted).T
    subspace = start_block
    for sweep in range(ITERS):
        image = jnp.dot(shifted.astype(jnp.float32), subspace.astype(jnp.float32), precision=lax.Precision.HIGHEST, preferred_element_type=jnp.float32)
        correlation = jnp.dot(image.T.astype(jnp.float32), image.astype(jnp.float32), precision=lax.Precision.HIGHEST, preferred_element_type=jnp.float32)
        lower_factor = jnp.linalg.cholesky(correlation)
        subspace = lax.linalg.triangular_solve(lower_factor, image, left_side=False, lower=True, transpose_a=True)
    pod_modes = jnp.dot(masked.astype(jnp.float32), subspace.astype(jnp.float32), precision=lax.Precision.HIGHEST, preferred_element_type=jnp.float32)
    return (pod_modes, upper_factor)
```

```python
import jax
import jax.numpy as jnp
from jax import lax
from jax.sharding import PartitionSpec as P

STEPS = 64
ITERS = 3
PASSES = 16
TILE = 128


def pack_upper(rows):
    width = rows.shape[1]
    pieces = []
    for i in range(width // TILE):
        lhs = rows[:, i * TILE:(i + 1) * TILE]
        rhs = rows[:, i * TILE:]
        pieces.append(
            lax.dot_general(lhs, rhs, (((0,), (0,)), ((), ())), preferred_element_type=jnp.float32)
        )
    return jnp.concatenate(pieces, axis=1)


def unpack_upper(packed, width):
    blocks = width // TILE
    upper_rows = []
    offset = 0
    for i in range(blocks):
        w = width - i * TILE
        piece = packed[:, offset:offset + w]
        offset += w
        upper_rows.append(jnp.pad(piece, ((0, 0), (i * TILE, 0))))
    upper = jnp.concatenate(upper_rows, axis=0)
    r = lax.broadcasted_iota(jnp.int32, (width, width), 0) // TILE
    c = lax.broadcasted_iota(jnp.int32, (width, width), 1) // TILE
    return jnp.where(r <= c, upper, upper.T)


def body(snapshots, lengths, start_block):
    rows = lax.all_to_all(snapshots, "snap", 0, 1, tiled=True)
    width = rows.shape[1]
    col_length = jnp.repeat(lengths, STEPS, total_repeat_length=width)
    columns = jnp.arange(width, dtype=jnp.int32)
    active = columns % STEPS < col_length
    masked = jnp.where(active[None, :], rows, jnp.zeros_like(rows))
    row_count = snapshots.shape[0] * lax.axis_size("dof")
    packed = lax.psum(pack_upper(masked), ("dof", "snap"))
    gram_sum = unpack_upper(packed, width)
    shifted = gram_sum / jnp.float32(row_count) + 0.05 * jnp.eye(width, dtype=jnp.float32)
    upper_factor = lax.linalg.cholesky(shifted, symmetrize_input=False).T
    contract = (((0,), (0,)), ((), ()))
    subspace = start_block
    for sweep in range(ITERS):
        image = jnp.dot(
            shifted, subspace, precision=lax.Precision.HIGHEST, preferred_element_type=jnp.float32
        )
        correlation = lax.dot_general(
            image, image, contract, precision=lax.Precision.HIGHEST, preferred_element_type=jnp.float32
        )
        lower_factor = jnp.linalg.cholesky(correlation)
        subspace = lax.linalg.triangular_solve(
            lower_factor, image, left_side=False, lower=True, transpose_a=True
        )
    pod_modes = jnp.dot(
        masked.astype(jnp.float32), subspace, precision=lax.Precision.HIGHEST,
        preferred_element_type=jnp.float32,
    )
    return (pod_modes, upper_factor)


def solution(mesh):
    placed = (P("dof", "snap"), P(), P())
    return jax.shard_map(
        body, mesh=mesh, in_specs=placed, out_specs=(P(("dof", "snap"), None), P()), check_vma=False
    )
```

```python
import jax
import jax.numpy as jnp
from jax import lax
from jax.sharding import PartitionSpec as P

STEPS = 64
ITERS = 3
PASSES = 16
TILE = 128


def pack_upper(rows):
    width = rows.shape[1]
    pieces = []
    for i in range(width // TILE):
        lhs = rows[:, i * TILE:(i + 1) * TILE]
        rhs = rows[:, i * TILE:]
        pieces.append(
            lax.dot_general(lhs, rhs, (((0,), (0,)), ((), ())), preferred_element_type=jnp.float32)
        )
    return jnp.concatenate(pieces, axis=1)


def unpack_upper(packed, width):
    blocks = width // TILE
    upper_rows = []
    offset = 0
    for i in range(blocks):
        w = width - i * TILE
        piece = packed[:, offset:offset + w]
        offset += w
        upper_rows.append(jnp.pad(piece, ((0, 0), (i * TILE, 0))))
    upper = jnp.concatenate(upper_rows, axis=0)
    r = lax.broadcasted_iota(jnp.int32, (width, width), 0) // TILE
    c = lax.broadcasted_iota(jnp.int32, (width, width), 1) // TILE
    return jnp.where(r <= c, upper, upper.T)


def all_reduce_a2a(x, axes):
    received = lax.all_to_all(x, axes, 0, 0, tiled=True)
    total = jnp.sum(received, axis=0, keepdims=True)
    spread = jnp.broadcast_to(total, x.shape)
    return lax.all_to_all(spread, axes, 0, 0, tiled=True)


def body(snapshots, lengths, start_block):
    rows = lax.all_to_all(snapshots, "snap", 0, 1, tiled=True)
    width = rows.shape[1]
    col_length = jnp.repeat(lengths, STEPS, total_repeat_length=width)
    columns = jnp.arange(width, dtype=jnp.int32)
    active = columns % STEPS < col_length
    masked = jnp.where(active[None, :], rows, jnp.zeros_like(rows))
    row_count = snapshots.shape[0] * lax.axis_size("dof")
    packed = all_reduce_a2a(pack_upper(masked), ("dof", "snap"))
    gram_sum = unpack_upper(packed, width)
    shifted = gram_sum / jnp.float32(row_count) + 0.05 * jnp.eye(width, dtype=jnp.float32)
    upper_factor = lax.linalg.cholesky(shifted, symmetrize_input=False).T
    contract = (((0,), (0,)), ((), ()))
    subspace = start_block
    for sweep in range(ITERS):
        image = jnp.dot(
            shifted, subspace, precision=lax.Precision.HIGHEST, preferred_element_type=jnp.float32
        )
        correlation = lax.dot_general(
            image, image, contract, precision=lax.Precision.HIGHEST, preferred_element_type=jnp.float32
        )
        lower_factor = jnp.linalg.cholesky(correlation)
        subspace = lax.linalg.triangular_solve(
            lower_factor, image, left_side=False, lower=True, transpose_a=True
        )
    pod_modes = jnp.dot(
        masked.astype(jnp.float32), subspace, precision=lax.Precision.HIGHEST,
        preferred_element_type=jnp.float32,
    )
    return (pod_modes, upper_factor)


def solution(mesh):
    placed = (P("dof", "snap"), P(), P())
    return jax.shard_map(
        body, mesh=mesh, in_specs=placed, out_specs=(P(("dof", "snap"), None), P()), check_vma=False
    )
```

```python
import functools
import jax
import jax.numpy as jnp
from jax import lax
from jax.experimental import pallas as pl
from jax.experimental.pallas import tpu as pltpu
from jax.sharding import PartitionSpec as P


HI = lax.Precision.HIGHEST
LEAF = 128


def mm(a, b):
    return jnp.dot(a, b, precision=HI, preferred_element_type=jnp.float32)


def mm_tn(a, b):
    return lax.dot_general(a, b, (((0,), (0,)), ((), ())), precision=HI, preferred_element_type=jnp.float32)


def mm_nt(a, b):
    return lax.dot_general(a, b, (((1,), (1,)), ((), ())), precision=HI, preferred_element_type=jnp.float32)


def leaf_chol_inv(a):
    n = a.shape[0]
    row = lax.broadcasted_iota(jnp.int32, (n, 2 * n), 0)
    lane = lax.broadcasted_iota(jnp.int32, (n, 2 * n), 1)
    eye = jnp.where(row == lane - n, 1.0, 0.0).astype(jnp.float32)
    m0 = jnp.where(lane < n, jnp.concatenate([a, a], axis=1), eye)
    row1 = lax.broadcasted_iota(jnp.int32, (n, 1), 0)
    lane1 = lax.broadcasted_iota(jnp.int32, (1, 2 * n), 1)

    def step(j, m):
        pick_row = row == j
        prow = jnp.sum(jnp.where(pick_row, m, 0.0), axis=0, keepdims=True)
        pivot = jnp.sum(jnp.where(lane1 == j, prow, 0.0), axis=1, keepdims=True)
        s = lax.rsqrt(pivot)
        nrow = prow * s
        col = jnp.sum(jnp.where(lane == j, m, 0.0), axis=1, keepdims=True)
        mult = jnp.where(row1 > j, col * s, 0.0)
        return jnp.where(pick_row, nrow, m - mult * nrow)

    m = lax.fori_loop(0, n, step, m0)
    r2 = lax.broadcasted_iota(jnp.int32, (n, n), 0)
    c2 = lax.broadcasted_iota(jnp.int32, (n, n), 1)
    u = jnp.where(r2 <= c2, m[:, :n], 0.0)
    w = m[:, n:]
    return u, w


def chol_inv(a, need_w):
    n = a.shape[0]
    if n <= LEAF:
        return leaf_chol_inv(a)
    h = n // 2
    u11, w11 = chol_inv(a[:h, :h], True)
    u12 = mm(w11, a[:h, h:])
    s = a[h:, h:] - mm_tn(u12, u12)
    u22, w22 = chol_inv(s, need_w)
    u = jnp.concatenate(
        [jnp.concatenate([u11, u12], axis=1),
         jnp.concatenate([jnp.zeros((h, h), jnp.float32), u22], axis=1)], axis=0)
    if not need_w:
        return u, None
    w21 = -mm(w22, mm_tn(u12, w11))
    w = jnp.concatenate(
        [jnp.concatenate([w11, jnp.zeros((h, h), jnp.float32)], axis=1),
         jnp.concatenate([w21, w22], axis=1)], axis=0)
    return u, w


def tail_kernel(iters, s_ref, b_ref, r_ref, out_ref):
    s = s_ref[...]
    u, _ = chol_inv(s, False)
    r_ref[...] = u
    blk = b_ref[...]
    for _ in range(iters):
        image = mm(s_ref[...], blk)
        corr = mm_tn(image, image)
        _, w = chol_inv(corr, True)
        blk = mm_nt(image, w)
    out_ref[...] = blk


def tail(shifted, start_block, iters):
    n = shifted.shape[0]
    k = start_block.shape[1]
    return pl.pallas_call(
        functools.partial(tail_kernel, iters),
        out_shape=(jax.ShapeDtypeStruct((n, n), jnp.float32), jax.ShapeDtypeStruct((n, k), jnp.float32)),
        in_specs=[pl.BlockSpec(memory_space=pltpu.VMEM)] * 2,
        out_specs=(pl.BlockSpec(memory_space=pltpu.VMEM),) * 2,
        compiler_params=pltpu.CompilerParams(vmem_limit_bytes=60 * 1024 * 1024),
    )(shifted, start_block)


STEPS = 64
ITERS = 3
PASSES = 16
TILE = 128


def pack_upper(rows):
    width = rows.shape[1]
    pieces = []
    for i in range(width // TILE):
        lhs = rows[:, i * TILE:(i + 1) * TILE]
        rhs = rows[:, i * TILE:]
        pieces.append(
            lax.dot_general(lhs, rhs, (((0,), (0,)), ((), ())), preferred_element_type=jnp.float32)
        )
    return jnp.concatenate(pieces, axis=1)


def unpack_upper(packed, width):
    blocks = width // TILE
    upper_rows = []
    offset = 0
    for i in range(blocks):
        w = width - i * TILE
        piece = packed[:, offset:offset + w]
        offset += w
        upper_rows.append(jnp.pad(piece, ((0, 0), (i * TILE, 0))))
    upper = jnp.concatenate(upper_rows, axis=0)
    r = lax.broadcasted_iota(jnp.int32, (width, width), 0) // TILE
    c = lax.broadcasted_iota(jnp.int32, (width, width), 1) // TILE
    return jnp.where(r <= c, upper, upper.T)


def all_reduce_a2a(x, axes):
    received = lax.all_to_all(x, axes, 0, 0, tiled=True)
    total = jnp.sum(received, axis=0, keepdims=True)
    spread = jnp.broadcast_to(total, x.shape)
    return lax.all_to_all(spread, axes, 0, 0, tiled=True)


def body(snapshots, lengths, start_block):
    rows = lax.all_to_all(snapshots, "snap", 0, 1, tiled=True)
    width = rows.shape[1]
    col_length = jnp.repeat(lengths, STEPS, total_repeat_length=width)
    columns = jnp.arange(width, dtype=jnp.int32)
    active = columns % STEPS < col_length
    masked = jnp.where(active[None, :], rows, jnp.zeros_like(rows))
    row_count = snapshots.shape[0] * lax.axis_size("dof")
    packed = all_reduce_a2a(pack_upper(masked), ("dof", "snap"))
    gram_sum = unpack_upper(packed, width)
    shifted = gram_sum / jnp.float32(row_count) + 0.05 * jnp.eye(width, dtype=jnp.float32)
    upper_factor, subspace = tail(shifted, start_block, ITERS)
    pod_modes = jnp.dot(
        masked.astype(jnp.float32), subspace, precision=lax.Precision.HIGHEST,
        preferred_element_type=jnp.float32,
    )
    return (pod_modes, upper_factor)


def solution(mesh):
    placed = (P("dof", "snap"), P(), P())
    return jax.shard_map(
        body, mesh=mesh, in_specs=placed, out_specs=(P(("dof", "snap"), None), P()), check_vma=False
    )
```

```python
import functools
import jax
import jax.numpy as jnp
from jax import lax
from jax.experimental import pallas as pl
from jax.experimental.pallas import tpu as pltpu
from jax.sharding import PartitionSpec as P


HI = lax.Precision.HIGHEST
LEAF = 128


def mm(a, b):
    return jnp.dot(a, b, precision=HI, preferred_element_type=jnp.float32)


def mm_tn(a, b):
    return lax.dot_general(a, b, (((0,), (0,)), ((), ())), precision=HI, preferred_element_type=jnp.float32)


def mm_nt(a, b):
    return lax.dot_general(a, b, (((1,), (1,)), ((), ())), precision=HI, preferred_element_type=jnp.float32)


def leaf_chol_inv(a):
    n = a.shape[0]
    row = lax.broadcasted_iota(jnp.int32, (n, 2 * n), 0)
    lane = lax.broadcasted_iota(jnp.int32, (n, 2 * n), 1)
    eye = jnp.where(row == lane - n, 1.0, 0.0).astype(jnp.float32)
    m0 = jnp.where(lane < n, jnp.concatenate([a, a], axis=1), eye)
    row1 = lax.broadcasted_iota(jnp.int32, (n, 1), 0)
    lane1 = lax.broadcasted_iota(jnp.int32, (1, 2 * n), 1)

    def step(j, m):
        pick_row = row == j
        prow = jnp.sum(jnp.where(pick_row, m, 0.0), axis=0, keepdims=True)
        pivot = jnp.sum(jnp.where(lane1 == j, prow, 0.0), axis=1, keepdims=True)
        s = lax.rsqrt(pivot)
        nrow = prow * s
        col = jnp.sum(jnp.where(lane == j, m, 0.0), axis=1, keepdims=True)
        mult = jnp.where(row1 > j, col * s, 0.0)
        return jnp.where(pick_row, nrow, m - mult * nrow)

    m = lax.fori_loop(0, n, step, m0)
    r2 = lax.broadcasted_iota(jnp.int32, (n, n), 0)
    c2 = lax.broadcasted_iota(jnp.int32, (n, n), 1)
    u = jnp.where(r2 <= c2, m[:, :n], 0.0)
    w = m[:, n:]
    return u, w


def chol_inv(a, need_w):
    n = a.shape[0]
    if n <= LEAF:
        return leaf_chol_inv(a)
    h = n // 2
    u11, w11 = chol_inv(a[:h, :h], True)
    u12 = mm(w11, a[:h, h:])
    s = a[h:, h:] - mm_tn(u12, u12)
    u22, w22 = chol_inv(s, need_w)
    u = jnp.concatenate(
        [jnp.concatenate([u11, u12], axis=1),
         jnp.concatenate([jnp.zeros((h, h), jnp.float32), u22], axis=1)], axis=0)
    if not need_w:
        return u, None
    w21 = -mm(w22, mm_tn(u12, w11))
    w = jnp.concatenate(
        [jnp.concatenate([w11, jnp.zeros((h, h), jnp.float32)], axis=1),
         jnp.concatenate([w21, w22], axis=1)], axis=0)
    return u, w


def chol_kernel(s_ref, r_ref):
    u, _ = chol_inv(s_ref[...], False)
    r_ref[...] = u


def sweep_kernel(iters, s_ref, b_ref, out_ref):
    blk = b_ref[...]
    for _ in range(iters):
        image = mm(s_ref[...], blk)
        corr = mm_tn(image, image)
        _, w = chol_inv(corr, True)
        blk = mm_nt(image, w)
    out_ref[...] = blk


VMEM_LIMIT = 60 * 1024 * 1024


def chol_call(shifted):
    n = shifted.shape[0]
    return pl.pallas_call(
        chol_kernel,
        out_shape=jax.ShapeDtypeStruct((n, n), jnp.float32),
        in_specs=[pl.BlockSpec(memory_space=pltpu.VMEM)],
        out_specs=pl.BlockSpec(memory_space=pltpu.VMEM),
        compiler_params=pltpu.CompilerParams(vmem_limit_bytes=VMEM_LIMIT),
    )(shifted)


def sweep_call(shifted, start_block, iters):
    n, k = start_block.shape
    return pl.pallas_call(
        functools.partial(sweep_kernel, iters),
        out_shape=jax.ShapeDtypeStruct((n, k), jnp.float32),
        in_specs=[pl.BlockSpec(memory_space=pltpu.VMEM)] * 2,
        out_specs=pl.BlockSpec(memory_space=pltpu.VMEM),
        compiler_params=pltpu.CompilerParams(vmem_limit_bytes=VMEM_LIMIT),
    )(shifted, start_block)


def tail_split(shifted, start_block, iters):
    n, k = start_block.shape
    core = lax.axis_index("dof") % 2

    def factor_side(a, b):
        return chol_call(a), jnp.zeros((n, k), jnp.float32)

    def sweep_side(a, b):
        return jnp.zeros((n, n), jnp.float32), sweep_call(a, b, iters)

    r_loc, b_loc = lax.cond(core == 0, factor_side, sweep_side, shifted, start_block)
    pairs = lax.axis_size("dof") // 2
    r_in = lax.ppermute(r_loc, "dof", [(2 * i, 2 * i + 1) for i in range(pairs)])
    b_in = lax.ppermute(b_loc, "dof", [(2 * i + 1, 2 * i) for i in range(pairs)])
    return r_loc + r_in, b_loc + b_in


STEPS = 64
ITERS = 3
PASSES = 16
TILE = 128


def pack_upper(rows):
    width = rows.shape[1]
    pieces = []
    for i in range(width // TILE):
        lhs = rows[:, i * TILE:(i + 1) * TILE]
        rhs = rows[:, i * TILE:]
        pieces.append(
            lax.dot_general(lhs, rhs, (((0,), (0,)), ((), ())), preferred_element_type=jnp.float32)
        )
    return jnp.concatenate(pieces, axis=1)


def unpack_upper(packed, width):
    blocks = width // TILE
    upper_rows = []
    offset = 0
    for i in range(blocks):
        w = width - i * TILE
        piece = packed[:, offset:offset + w]
        offset += w
        upper_rows.append(jnp.pad(piece, ((0, 0), (i * TILE, 0))))
    upper = jnp.concatenate(upper_rows, axis=0)
    r = lax.broadcasted_iota(jnp.int32, (width, width), 0) // TILE
    c = lax.broadcasted_iota(jnp.int32, (width, width), 1) // TILE
    return jnp.where(r <= c, upper, upper.T)


def all_reduce_a2a(x, axes):
    received = lax.all_to_all(x, axes, 0, 0, tiled=True)
    total = jnp.sum(received, axis=0, keepdims=True)
    spread = jnp.broadcast_to(total, x.shape)
    return lax.all_to_all(spread, axes, 0, 0, tiled=True)


def body(snapshots, lengths, start_block):
    rows = lax.all_to_all(snapshots, "snap", 0, 1, tiled=True)
    width = rows.shape[1]
    col_length = jnp.repeat(lengths, STEPS, total_repeat_length=width)
    columns = jnp.arange(width, dtype=jnp.int32)
    active = columns % STEPS < col_length
    masked = jnp.where(active[None, :], rows, jnp.zeros_like(rows))
    row_count = snapshots.shape[0] * lax.axis_size("dof")
    packed = all_reduce_a2a(pack_upper(masked), ("dof", "snap"))
    gram_sum = unpack_upper(packed, width)
    shifted = gram_sum / jnp.float32(row_count) + 0.05 * jnp.eye(width, dtype=jnp.float32)
    upper_factor, subspace = tail_split(shifted, start_block, ITERS)
    pod_modes = jnp.dot(
        masked.astype(jnp.float32), subspace, precision=lax.Precision.HIGHEST,
        preferred_element_type=jnp.float32,
    )
    return (pod_modes, upper_factor)


def solution(mesh):
    placed = (P("dof", "snap"), P(), P())
    return jax.shard_map(
        body, mesh=mesh, in_specs=placed, out_specs=(P(("dof", "snap"), None), P()), check_vma=False
    )
```

```python
import functools
import jax
import jax.numpy as jnp
from jax import lax
from jax.experimental import pallas as pl
from jax.experimental.pallas import tpu as pltpu
from jax.sharding import PartitionSpec as P


HI = lax.Precision.HIGHEST
LEAF = 128


def mm(a, b):
    return jnp.dot(a, b, precision=HI, preferred_element_type=jnp.float32)


def mm_tn(a, b):
    return lax.dot_general(a, b, (((0,), (0,)), ((), ())), precision=HI, preferred_element_type=jnp.float32)


def mm_nt(a, b):
    return lax.dot_general(a, b, (((1,), (1,)), ((), ())), precision=HI, preferred_element_type=jnp.float32)


def leaf_chol_inv(a):
    n = a.shape[0]
    row = lax.broadcasted_iota(jnp.int32, (n, 2 * n), 0)
    lane = lax.broadcasted_iota(jnp.int32, (n, 2 * n), 1)
    eye = jnp.where(row == lane - n, 1.0, 0.0).astype(jnp.float32)
    m0 = jnp.where(lane < n, jnp.concatenate([a, a], axis=1), eye)
    row1 = lax.broadcasted_iota(jnp.int32, (n, 1), 0)
    lane1 = lax.broadcasted_iota(jnp.int32, (1, 2 * n), 1)

    def step(j, m):
        pick_row = row == j
        prow = jnp.sum(jnp.where(pick_row, m, 0.0), axis=0, keepdims=True)
        pivot = jnp.sum(jnp.where(lane1 == j, prow, 0.0), axis=1, keepdims=True)
        s = lax.rsqrt(pivot)
        nrow = prow * s
        col = jnp.sum(jnp.where(lane == j, m, 0.0), axis=1, keepdims=True)
        mult = jnp.where(row1 > j, col * s, 0.0)
        return jnp.where(pick_row, nrow, m - mult * nrow)

    m = lax.fori_loop(0, n, step, m0)
    r2 = lax.broadcasted_iota(jnp.int32, (n, n), 0)
    c2 = lax.broadcasted_iota(jnp.int32, (n, n), 1)
    u = jnp.where(r2 <= c2, m[:, :n], 0.0)
    w = m[:, n:]
    return u, w


def chol_inv(a, need_w):
    n = a.shape[0]
    if n <= LEAF:
        return leaf_chol_inv(a)
    h = n // 2
    u11, w11 = chol_inv(a[:h, :h], True)
    u12 = mm(w11, a[:h, h:])
    s = a[h:, h:] - mm_tn(u12, u12)
    u22, w22 = chol_inv(s, need_w)
    u = jnp.concatenate(
        [jnp.concatenate([u11, u12], axis=1),
         jnp.concatenate([jnp.zeros((h, h), jnp.float32), u22], axis=1)], axis=0)
    if not need_w:
        return u, None
    w21 = -mm(w22, mm_tn(u12, w11))
    w = jnp.concatenate(
        [jnp.concatenate([w11, jnp.zeros((h, h), jnp.float32)], axis=1),
         jnp.concatenate([w21, w22], axis=1)], axis=0)
    return u, w


def chol_kernel(s_ref, r_ref):
    u, _ = chol_inv(s_ref[...], False)
    r_ref[...] = u


def sweep_kernel(iters, s_ref, b_ref, out_ref):
    blk = b_ref[...]
    for _ in range(iters):
        image = mm(s_ref[...], blk)
        corr = mm_tn(image, image)
        _, w = chol_inv(corr, True)
        blk = mm_nt(image, w)
    out_ref[...] = blk


VMEM_LIMIT = 60 * 1024 * 1024


def chol_call(shifted):
    n = shifted.shape[0]
    return pl.pallas_call(
        chol_kernel,
        out_shape=jax.ShapeDtypeStruct((n, n), jnp.float32),
        in_specs=[pl.BlockSpec(memory_space=pltpu.VMEM)],
        out_specs=pl.BlockSpec(memory_space=pltpu.VMEM),
        compiler_params=pltpu.CompilerParams(vmem_limit_bytes=VMEM_LIMIT),
    )(shifted)


def sweep_call(shifted, start_block, iters):
    n, k = start_block.shape
    return pl.pallas_call(
        functools.partial(sweep_kernel, iters),
        out_shape=jax.ShapeDtypeStruct((n, k), jnp.float32),
        in_specs=[pl.BlockSpec(memory_space=pltpu.VMEM)] * 2,
        out_specs=pl.BlockSpec(memory_space=pltpu.VMEM),
        compiler_params=pltpu.CompilerParams(vmem_limit_bytes=VMEM_LIMIT),
    )(shifted, start_block)


def tail_split(shifted, start_block, iters):
    n, k = start_block.shape
    core = lax.axis_index("dof") % 2

    def factor_side(a, b):
        return chol_call(a), jnp.zeros((n, k), jnp.float32)

    def sweep_side(a, b):
        return jnp.zeros((n, n), jnp.float32), sweep_call(a, b, iters)

    r_loc, b_loc = lax.cond(core == 0, factor_side, sweep_side, shifted, start_block)
    pairs = lax.axis_size("dof") // 2
    r_in = lax.ppermute(r_loc, "dof", [(2 * i, 2 * i + 1) for i in range(pairs)])
    b_in = lax.ppermute(b_loc, "dof", [(2 * i + 1, 2 * i) for i in range(pairs)])
    return r_loc + r_in, b_loc + b_in


STEPS = 64
ITERS = 3
PASSES = 16
TILE = 128


def pack_upper(rows):
    width = rows.shape[1]
    pieces = []
    for i in range(width // TILE):
        lhs = rows[:, i * TILE:(i + 1) * TILE]
        rhs = rows[:, i * TILE:]
        pieces.append(
            lax.dot_general(lhs, rhs, (((0,), (0,)), ((), ())), preferred_element_type=jnp.float32)
        )
    return jnp.concatenate(pieces, axis=1)


def unpack_upper(packed, width):
    blocks = width // TILE
    upper_rows = []
    offset = 0
    for i in range(blocks):
        w = width - i * TILE
        piece = packed[:, offset:offset + w]
        offset += w
        upper_rows.append(jnp.pad(piece, ((0, 0), (i * TILE, 0))))
    upper = jnp.concatenate(upper_rows, axis=0)
    r = lax.broadcasted_iota(jnp.int32, (width, width), 0) // TILE
    c = lax.broadcasted_iota(jnp.int32, (width, width), 1) // TILE
    return jnp.where(r <= c, upper, upper.T)


def all_reduce_a2a(x, axes):
    rows, cols = x.shape
    half = rows // 2
    ndof = lax.axis_size("dof")
    nsnap = lax.axis_size("snap")
    core = lax.axis_index("dof") % 2
    swap = [(i, i ^ 1) for i in range(ndof)]
    mine = lax.dynamic_slice_in_dim(x, core * half, half, 0)
    theirs = lax.dynamic_slice_in_dim(x, (1 - core) * half, half, 0)
    own = mine + lax.ppermute(theirs, "dof", swap)
    stacked = jnp.concatenate([own[:, :cols // 2], own[:, cols // 2:]], axis=0)
    received = lax.all_to_all(stacked, axes, 0, 0, tiled=True)
    by_core = received.reshape(ndof // 2, 2, nsnap, cols // 2).sum(axis=(0, 2))
    spread = jnp.broadcast_to(by_core[None, :, None, :], (ndof // 2, 2, nsnap, cols // 2))
    gathered = lax.all_to_all(spread.reshape(rows, cols // 2), axes, 0, 0, tiled=True)
    own_total = jnp.concatenate([gathered[:half], gathered[half:]], axis=1)
    other_total = lax.ppermute(own_total, "dof", swap)
    first = jnp.where(core == 0, own_total, other_total)
    second = jnp.where(core == 0, other_total, own_total)
    return jnp.concatenate([first, second], axis=0)


def body(snapshots, lengths, start_block):
    rows = lax.all_to_all(snapshots, "snap", 0, 1, tiled=True)
    width = rows.shape[1]
    col_length = jnp.repeat(lengths, STEPS, total_repeat_length=width)
    columns = jnp.arange(width, dtype=jnp.int32)
    active = columns % STEPS < col_length
    masked = jnp.where(active[None, :], rows, jnp.zeros_like(rows))
    row_count = snapshots.shape[0] * lax.axis_size("dof")
    packed = all_reduce_a2a(pack_upper(masked), ("dof", "snap"))
    gram_sum = unpack_upper(packed, width)
    shifted = gram_sum / jnp.float32(row_count) + 0.05 * jnp.eye(width, dtype=jnp.float32)
    upper_factor, subspace = tail_split(shifted, start_block, ITERS)
    pod_modes = jnp.dot(
        masked.astype(jnp.float32), subspace, precision=lax.Precision.HIGHEST,
        preferred_element_type=jnp.float32,
    )
    return (pod_modes, upper_factor)


def solution(mesh):
    placed = (P("dof", "snap"), P(), P())
    return jax.shard_map(
        body, mesh=mesh, in_specs=placed, out_specs=(P(("dof", "snap"), None), P()), check_vma=False
    )
```

```python
import functools
import jax
import jax.numpy as jnp
from jax import lax
from jax.experimental import pallas as pl
from jax.experimental.pallas import tpu as pltpu
from jax.sharding import PartitionSpec as P


HI = lax.Precision.HIGHEST
LEAF = 128


def mm(a, b):
    return jnp.dot(a, b, precision=HI, preferred_element_type=jnp.float32)


def mm_tn(a, b):
    return lax.dot_general(a, b, (((0,), (0,)), ((), ())), precision=HI, preferred_element_type=jnp.float32)


def mm_nt(a, b):
    return lax.dot_general(a, b, (((1,), (1,)), ((), ())), precision=HI, preferred_element_type=jnp.float32)


def leaf_chol_inv(a):
    n = a.shape[0]
    row = lax.broadcasted_iota(jnp.int32, (n, 2 * n), 0)
    lane = lax.broadcasted_iota(jnp.int32, (n, 2 * n), 1)
    eye = jnp.where(row == lane - n, 1.0, 0.0).astype(jnp.float32)
    m0 = jnp.where(lane < n, jnp.concatenate([a, a], axis=1), eye)
    row1 = lax.broadcasted_iota(jnp.int32, (n, 1), 0)
    lane1 = lax.broadcasted_iota(jnp.int32, (1, 2 * n), 1)

    def step(j, m):
        pick_row = row == j
        prow = jnp.sum(jnp.where(pick_row, m, 0.0), axis=0, keepdims=True)
        pivot = jnp.sum(jnp.where(lane1 == j, prow, 0.0), axis=1, keepdims=True)
        s = lax.rsqrt(pivot)
        nrow = prow * s
        col = jnp.sum(jnp.where(lane == j, m, 0.0), axis=1, keepdims=True)
        mult = jnp.where(row1 > j, col * s, 0.0)
        return jnp.where(pick_row, nrow, m - mult * nrow)

    m = lax.fori_loop(0, n, step, m0)
    r2 = lax.broadcasted_iota(jnp.int32, (n, n), 0)
    c2 = lax.broadcasted_iota(jnp.int32, (n, n), 1)
    u = jnp.where(r2 <= c2, m[:, :n], 0.0)
    w = m[:, n:]
    return u, w


def chol_inv(a, need_w):
    n = a.shape[0]
    if n <= LEAF:
        return leaf_chol_inv(a)
    h = n // 2
    u11, w11 = chol_inv(a[:h, :h], True)
    u12 = mm(w11, a[:h, h:])
    s = a[h:, h:] - mm_tn(u12, u12)
    u22, w22 = chol_inv(s, need_w)
    u = jnp.concatenate(
        [jnp.concatenate([u11, u12], axis=1),
         jnp.concatenate([jnp.zeros((h, h), jnp.float32), u22], axis=1)], axis=0)
    if not need_w:
        return u, None
    w21 = -mm(w22, mm_tn(u12, w11))
    w = jnp.concatenate(
        [jnp.concatenate([w11, jnp.zeros((h, h), jnp.float32)], axis=1),
         jnp.concatenate([w21, w22], axis=1)], axis=0)
    return u, w


def build_shifted(p_ref, sref, scale):
    n = sref.shape[0]
    eye = jnp.where(lax.broadcasted_iota(jnp.int32, (TILE, TILE), 0)
                    == lax.broadcasted_iota(jnp.int32, (TILE, TILE), 1), 0.05, 0.0).astype(jnp.float32)
    offset = 0
    for i in range(n // TILE):
        for j in range(i, n // TILE):
            c0 = offset + (j - i) * TILE
            blk = p_ref[:, c0:c0 + TILE] * scale
            if i == j:
                sref[i * TILE:(i + 1) * TILE, j * TILE:(j + 1) * TILE] = blk + eye
            else:
                sref[i * TILE:(i + 1) * TILE, j * TILE:(j + 1) * TILE] = blk
                sref[j * TILE:(j + 1) * TILE, i * TILE:(i + 1) * TILE] = jnp.transpose(blk)
        offset += n - i * TILE


def chol_kernel(scale, p_ref, r_ref, sref):
    build_shifted(p_ref, sref, scale)
    u, _ = chol_inv(sref[...], False)
    r_ref[...] = u


def sweep_kernel(iters, scale, p_ref, b_ref, out_ref, sref):
    build_shifted(p_ref, sref, scale)
    blk = b_ref[...]
    for _ in range(iters):
        image = mm(sref[...], blk)
        corr = mm_tn(image, image)
        _, w = chol_inv(corr, True)
        blk = mm_nt(image, w)
    out_ref[...] = blk


VMEM_LIMIT = 60 * 1024 * 1024


def chol_call(packed, n, scale):
    return pl.pallas_call(
        functools.partial(chol_kernel, scale),
        out_shape=jax.ShapeDtypeStruct((n, n), jnp.float32),
        in_specs=[pl.BlockSpec(memory_space=pltpu.VMEM)],
        out_specs=pl.BlockSpec(memory_space=pltpu.VMEM),
        scratch_shapes=[pltpu.VMEM((n, n), jnp.float32)],
        compiler_params=pltpu.CompilerParams(vmem_limit_bytes=VMEM_LIMIT),
    )(packed)


def sweep_call(packed, start_block, iters, scale):
    n, k = start_block.shape
    return pl.pallas_call(
        functools.partial(sweep_kernel, iters, scale),
        out_shape=jax.ShapeDtypeStruct((n, k), jnp.float32),
        in_specs=[pl.BlockSpec(memory_space=pltpu.VMEM)] * 2,
        out_specs=pl.BlockSpec(memory_space=pltpu.VMEM),
        scratch_shapes=[pltpu.VMEM((n, n), jnp.float32)],
        compiler_params=pltpu.CompilerParams(vmem_limit_bytes=VMEM_LIMIT),
    )(packed, start_block)


def tail_split(packed, start_block, iters, scale):
    n, k = start_block.shape
    core = lax.axis_index("dof") % 2

    def factor_side(a, b):
        return chol_call(a, n, scale), jnp.zeros((n, k), jnp.float32)

    def sweep_side(a, b):
        return jnp.zeros((n, n), jnp.float32), sweep_call(a, b, iters, scale)

    r_loc, b_loc = lax.cond(core == 0, factor_side, sweep_side, packed, start_block)
    pairs = lax.axis_size("dof") // 2
    r_in = lax.ppermute(r_loc, "dof", [(2 * i, 2 * i + 1) for i in range(pairs)])
    b_in = lax.ppermute(b_loc, "dof", [(2 * i + 1, 2 * i) for i in range(pairs)])
    return r_loc + r_in, b_loc + b_in


STEPS = 64
ITERS = 3
PASSES = 16
TILE = 128


def pack_upper(rows):
    width = rows.shape[1]
    pieces = []
    for i in range(width // TILE):
        lhs = rows[:, i * TILE:(i + 1) * TILE]
        rhs = rows[:, i * TILE:]
        pieces.append(
            lax.dot_general(lhs, rhs, (((0,), (0,)), ((), ())), preferred_element_type=jnp.float32)
        )
    return jnp.concatenate(pieces, axis=1)


def all_reduce_a2a(x, axes):
    rows, cols = x.shape
    half = rows // 2
    ndof = lax.axis_size("dof")
    nsnap = lax.axis_size("snap")
    core = lax.axis_index("dof") % 2
    swap = [(i, i ^ 1) for i in range(ndof)]
    mine = lax.dynamic_slice_in_dim(x, core * half, half, 0)
    theirs = lax.dynamic_slice_in_dim(x, (1 - core) * half, half, 0)
    own = mine + lax.ppermute(theirs, "dof", swap)
    stacked = jnp.concatenate([own[:, :cols // 2], own[:, cols // 2:]], axis=0)
    received = lax.all_to_all(stacked, axes, 0, 0, tiled=True)
    by_core = received.reshape(ndof // 2, 2, nsnap, cols // 2).sum(axis=(0, 2))
    spread = jnp.broadcast_to(by_core[None, :, None, :], (ndof // 2, 2, nsnap, cols // 2))
    gathered = lax.all_to_all(spread.reshape(rows, cols // 2), axes, 0, 0, tiled=True)
    own_total = jnp.concatenate([gathered[:half], gathered[half:]], axis=1)
    other_total = lax.ppermute(own_total, "dof", swap)
    first = jnp.where(core == 0, own_total, other_total)
    second = jnp.where(core == 0, other_total, own_total)
    return jnp.concatenate([first, second], axis=0)


def body(snapshots, lengths, start_block):
    rows = lax.all_to_all(snapshots, "snap", 0, 1, tiled=True)
    width = rows.shape[1]
    col_length = jnp.repeat(lengths, STEPS, total_repeat_length=width)
    columns = jnp.arange(width, dtype=jnp.int32)
    active = columns % STEPS < col_length
    masked = jnp.where(active[None, :], rows, jnp.zeros_like(rows))
    row_count = snapshots.shape[0] * lax.axis_size("dof")
    packed = all_reduce_a2a(pack_upper(masked), ("dof", "snap"))
    upper_factor, subspace = tail_split(packed, start_block, ITERS, 1.0 / row_count)
    pod_modes = jnp.dot(
        masked.astype(jnp.float32), subspace, precision=lax.Precision.HIGHEST,
        preferred_element_type=jnp.float32,
    )
    return (pod_modes, upper_factor)


def solution(mesh):
    placed = (P("dof", "snap"), P(), P())
    return jax.shard_map(
        body, mesh=mesh, in_specs=placed, out_specs=(P(("dof", "snap"), None), P()), check_vma=False
    )
```

```python
import functools
import jax
import jax.numpy as jnp
from jax import lax
from jax.experimental import pallas as pl
from jax.experimental.pallas import tpu as pltpu
from jax.sharding import PartitionSpec as P


HI = lax.Precision.HIGHEST
LEAF = 128


def mm(a, b):
    return jnp.dot(a, b, precision=HI, preferred_element_type=jnp.float32)


def mm_tn(a, b):
    return lax.dot_general(a, b, (((0,), (0,)), ((), ())), precision=HI, preferred_element_type=jnp.float32)


def mm_nt(a, b):
    return lax.dot_general(a, b, (((1,), (1,)), ((), ())), precision=HI, preferred_element_type=jnp.float32)


def leaf_chol_inv(a):
    n = a.shape[0]
    row = lax.broadcasted_iota(jnp.int32, (n, 2 * n), 0)
    lane = lax.broadcasted_iota(jnp.int32, (n, 2 * n), 1)
    eye = jnp.where(row == lane - n, 1.0, 0.0).astype(jnp.float32)
    m0 = jnp.where(lane < n, jnp.concatenate([a, a], axis=1), eye)
    r2 = lax.broadcasted_iota(jnp.int32, (n, n), 0)
    c2 = lax.broadcasted_iota(jnp.int32, (n, n), 1)
    d0 = jnp.sum(jnp.where(r2 == c2, a, 0.0), axis=0, keepdims=True)
    row1 = lax.broadcasted_iota(jnp.int32, (n, 1), 0)
    lane1 = lax.broadcasted_iota(jnp.int32, (1, n), 1)

    def step(j, carry):
        m, d = carry
        pivot = jnp.sum(jnp.where(lane1 == j, d, 0.0), axis=1, keepdims=True)
        s = lax.rsqrt(pivot)
        pick_row = row == j
        prow = jnp.sum(jnp.where(pick_row, m, 0.0), axis=0, keepdims=True)
        col = jnp.sum(jnp.where(lane[:, :n] == j, m[:, :n], 0.0), axis=1, keepdims=True)
        nrow = prow * s
        mult = jnp.where(row1 > j, col * s, 0.0)
        head = nrow[:, :n]
        return jnp.where(pick_row, nrow, m - mult * nrow), d - head * head

    m, _ = lax.fori_loop(0, n, step, (m0, d0), unroll=2)
    u = jnp.where(r2 <= c2, m[:, :n], 0.0)
    w = m[:, n:]
    return u, w


def chol_inv(a, need_w):
    n = a.shape[0]
    if n <= LEAF:
        return leaf_chol_inv(a)
    h = n // 2
    u11, w11 = chol_inv(a[:h, :h], True)
    u12 = mm(w11, a[:h, h:])
    s = a[h:, h:] - mm_tn(u12, u12)
    u22, w22 = chol_inv(s, need_w)
    u = jnp.concatenate(
        [jnp.concatenate([u11, u12], axis=1),
         jnp.concatenate([jnp.zeros((h, h), jnp.float32), u22], axis=1)], axis=0)
    if not need_w:
        return u, None
    w21 = -mm(w22, mm_tn(u12, w11))
    w = jnp.concatenate(
        [jnp.concatenate([w11, jnp.zeros((h, h), jnp.float32)], axis=1),
         jnp.concatenate([w21, w22], axis=1)], axis=0)
    return u, w


def build_shifted(p_ref, sref, scale):
    n = sref.shape[0]
    eye = jnp.where(lax.broadcasted_iota(jnp.int32, (TILE, TILE), 0)
                    == lax.broadcasted_iota(jnp.int32, (TILE, TILE), 1), 0.05, 0.0).astype(jnp.float32)
    offset = 0
    for i in range(n // TILE):
        for j in range(i, n // TILE):
            c0 = offset + (j - i) * TILE
            blk = p_ref[:, c0:c0 + TILE] * scale
            if i == j:
                sref[i * TILE:(i + 1) * TILE, j * TILE:(j + 1) * TILE] = blk + eye
            else:
                sref[i * TILE:(i + 1) * TILE, j * TILE:(j + 1) * TILE] = blk
                sref[j * TILE:(j + 1) * TILE, i * TILE:(i + 1) * TILE] = jnp.transpose(blk)
        offset += n - i * TILE


def chol_kernel(scale, p_ref, r_ref, sref):
    build_shifted(p_ref, sref, scale)
    u, _ = chol_inv(sref[...], False)
    r_ref[...] = u


def sweep_kernel(iters, scale, p_ref, b_ref, out_ref, sref):
    build_shifted(p_ref, sref, scale)
    blk = b_ref[...]
    for _ in range(iters):
        image = mm(sref[...], blk)
        corr = mm_tn(image, image)
        _, w = chol_inv(corr, True)
        blk = mm_nt(image, w)
    out_ref[...] = blk


VMEM_LIMIT = 60 * 1024 * 1024


def chol_call(packed, n, scale):
    return pl.pallas_call(
        functools.partial(chol_kernel, scale),
        out_shape=jax.ShapeDtypeStruct((n, n), jnp.float32),
        in_specs=[pl.BlockSpec(memory_space=pltpu.VMEM)],
        out_specs=pl.BlockSpec(memory_space=pltpu.VMEM),
        scratch_shapes=[pltpu.VMEM((n, n), jnp.float32)],
        compiler_params=pltpu.CompilerParams(vmem_limit_bytes=VMEM_LIMIT),
    )(packed)


def sweep_call(packed, start_block, iters, scale):
    n, k = start_block.shape
    return pl.pallas_call(
        functools.partial(sweep_kernel, iters, scale),
        out_shape=jax.ShapeDtypeStruct((n, k), jnp.float32),
        in_specs=[pl.BlockSpec(memory_space=pltpu.VMEM)] * 2,
        out_specs=pl.BlockSpec(memory_space=pltpu.VMEM),
        scratch_shapes=[pltpu.VMEM((n, n), jnp.float32)],
        compiler_params=pltpu.CompilerParams(vmem_limit_bytes=VMEM_LIMIT),
    )(packed, start_block)


def tail_split(packed, start_block, iters, scale):
    n, k = start_block.shape
    core = lax.axis_index("dof") % 2

    def factor_side(a, b):
        return chol_call(a, n, scale), jnp.zeros((n, k), jnp.float32)

    def sweep_side(a, b):
        return jnp.zeros((n, n), jnp.float32), sweep_call(a, b, iters, scale)

    r_loc, b_loc = lax.cond(core == 0, factor_side, sweep_side, packed, start_block)
    pairs = lax.axis_size("dof") // 2
    r_in = lax.ppermute(r_loc, "dof", [(2 * i, 2 * i + 1) for i in range(pairs)])
    b_in = lax.ppermute(b_loc, "dof", [(2 * i + 1, 2 * i) for i in range(pairs)])
    return r_loc + r_in, b_loc + b_in


STEPS = 64
ITERS = 3
PASSES = 16
TILE = 128


def pack_upper(rows):
    width = rows.shape[1]
    pieces = []
    for i in range(width // TILE):
        lhs = rows[:, i * TILE:(i + 1) * TILE]
        rhs = rows[:, i * TILE:]
        pieces.append(
            lax.dot_general(lhs, rhs, (((0,), (0,)), ((), ())), preferred_element_type=jnp.float32)
        )
    return jnp.concatenate(pieces, axis=1)


def all_reduce_a2a(x, axes):
    rows, cols = x.shape
    half = rows // 2
    ndof = lax.axis_size("dof")
    nsnap = lax.axis_size("snap")
    core = lax.axis_index("dof") % 2
    swap = [(i, i ^ 1) for i in range(ndof)]
    mine = lax.dynamic_slice_in_dim(x, core * half, half, 0)
    theirs = lax.dynamic_slice_in_dim(x, (1 - core) * half, half, 0)
    own = mine + lax.ppermute(theirs, "dof", swap)
    stacked = jnp.concatenate([own[:, :cols // 2], own[:, cols // 2:]], axis=0)
    received = lax.all_to_all(stacked, axes, 0, 0, tiled=True)
    by_core = received.reshape(ndof // 2, 2, nsnap, cols // 2).sum(axis=(0, 2))
    spread = jnp.broadcast_to(by_core[None, :, None, :], (ndof // 2, 2, nsnap, cols // 2))
    gathered = lax.all_to_all(spread.reshape(rows, cols // 2), axes, 0, 0, tiled=True)
    own_total = jnp.concatenate([gathered[:half], gathered[half:]], axis=1)
    other_total = lax.ppermute(own_total, "dof", swap)
    first = jnp.where(core == 0, own_total, other_total)
    second = jnp.where(core == 0, other_total, own_total)
    return jnp.concatenate([first, second], axis=0)


def body(snapshots, lengths, start_block):
    rows = lax.all_to_all(snapshots, "snap", 0, 1, tiled=True)
    width = rows.shape[1]
    col_length = jnp.repeat(lengths, STEPS, total_repeat_length=width)
    columns = jnp.arange(width, dtype=jnp.int32)
    active = columns % STEPS < col_length
    masked = jnp.where(active[None, :], rows, jnp.zeros_like(rows))
    row_count = snapshots.shape[0] * lax.axis_size("dof")
    packed = all_reduce_a2a(pack_upper(masked), ("dof", "snap"))
    upper_factor, subspace = tail_split(packed, start_block, ITERS, 1.0 / row_count)
    pod_modes = jnp.dot(
        masked.astype(jnp.float32), subspace, precision=lax.Precision.HIGHEST,
        preferred_element_type=jnp.float32,
    )
    return (pod_modes, upper_factor)


def solution(mesh):
    placed = (P("dof", "snap"), P(), P())
    return jax.shard_map(
        body, mesh=mesh, in_specs=placed, out_specs=(P(("dof", "snap"), None), P()), check_vma=False
    )
```

```python
import functools
import jax
import jax.numpy as jnp
from jax import lax
from jax.experimental import pallas as pl
from jax.experimental.pallas import tpu as pltpu
from jax.sharding import PartitionSpec as P


HI = lax.Precision.HIGHEST
LEAF = 128


def mm(a, b):
    return jnp.dot(a, b, precision=HI, preferred_element_type=jnp.float32)


def mm_tn(a, b):
    return lax.dot_general(a, b, (((0,), (0,)), ((), ())), precision=HI, preferred_element_type=jnp.float32)


def mm_nt(a, b):
    return lax.dot_general(a, b, (((1,), (1,)), ((), ())), precision=HI, preferred_element_type=jnp.float32)


def leaf_chol_inv(a):
    n = a.shape[0]
    row = lax.broadcasted_iota(jnp.int32, (n, 2 * n), 0)
    lane = lax.broadcasted_iota(jnp.int32, (n, 2 * n), 1)
    eye = jnp.where(row == lane - n, 1.0, 0.0).astype(jnp.float32)
    m0 = jnp.where(lane < n, jnp.concatenate([a, a], axis=1), eye)
    r2 = lax.broadcasted_iota(jnp.int32, (n, n), 0)
    c2 = lax.broadcasted_iota(jnp.int32, (n, n), 1)
    d0 = jnp.sum(jnp.where(r2 == c2, a, 0.0), axis=0, keepdims=True)
    row1 = lax.broadcasted_iota(jnp.int32, (n, 1), 0)
    lane1 = lax.broadcasted_iota(jnp.int32, (1, n), 1)

    def step(j, carry):
        m, d = carry
        pivot = jnp.sum(jnp.where(lane1 == j, d, 0.0), axis=1, keepdims=True)
        s = lax.rsqrt(pivot)
        pick_row = row == j
        prow = jnp.sum(jnp.where(pick_row, m, 0.0), axis=0, keepdims=True)
        col = jnp.sum(jnp.where(lane[:, :n] == j, m[:, :n], 0.0), axis=1, keepdims=True)
        nrow = prow * s
        mult = jnp.where(row1 > j, col * s, 0.0)
        head = nrow[:, :n]
        return jnp.where(pick_row, nrow, m - mult * nrow), d - head * head

    m, _ = lax.fori_loop(0, n, step, (m0, d0), unroll=4)
    u = jnp.where(r2 <= c2, m[:, :n], 0.0)
    w = m[:, n:]
    return u, w


def chol_inv(a, need_w):
    n = a.shape[0]
    if n <= LEAF:
        return leaf_chol_inv(a)
    h = n // 2
    u11, w11 = chol_inv(a[:h, :h], True)
    u12 = mm(w11, a[:h, h:])
    s = a[h:, h:] - mm_tn(u12, u12)
    u22, w22 = chol_inv(s, need_w)
    u = jnp.concatenate(
        [jnp.concatenate([u11, u12], axis=1),
         jnp.concatenate([jnp.zeros((h, h), jnp.float32), u22], axis=1)], axis=0)
    if not need_w:
        return u, None
    w21 = -mm(w22, mm_tn(u12, w11))
    w = jnp.concatenate(
        [jnp.concatenate([w11, jnp.zeros((h, h), jnp.float32)], axis=1),
         jnp.concatenate([w21, w22], axis=1)], axis=0)
    return u, w


def build_shifted(p_ref, sref, scale):
    n = sref.shape[0]
    eye = jnp.where(lax.broadcasted_iota(jnp.int32, (TILE, TILE), 0)
                    == lax.broadcasted_iota(jnp.int32, (TILE, TILE), 1), 0.05, 0.0).astype(jnp.float32)
    offset = 0
    for i in range(n // TILE):
        for j in range(i, n // TILE):
            c0 = offset + (j - i) * TILE
            blk = p_ref[:, c0:c0 + TILE] * scale
            if i == j:
                sref[i * TILE:(i + 1) * TILE, j * TILE:(j + 1) * TILE] = blk + eye
            else:
                sref[i * TILE:(i + 1) * TILE, j * TILE:(j + 1) * TILE] = blk
                sref[j * TILE:(j + 1) * TILE, i * TILE:(i + 1) * TILE] = jnp.transpose(blk)
        offset += n - i * TILE


def chol_kernel(scale, p_ref, r_ref, sref):
    build_shifted(p_ref, sref, scale)
    u, _ = chol_inv(sref[...], False)
    r_ref[...] = u


def sweep_kernel(iters, scale, p_ref, b_ref, out_ref, sref):
    build_shifted(p_ref, sref, scale)
    blk = b_ref[...]
    for _ in range(iters):
        image = mm(sref[...], blk)
        corr = mm_tn(image, image)
        _, w = chol_inv(corr, True)
        blk = mm_nt(image, w)
    out_ref[...] = blk


VMEM_LIMIT = 60 * 1024 * 1024


def chol_call(packed, n, scale):
    return pl.pallas_call(
        functools.partial(chol_kernel, scale),
        out_shape=jax.ShapeDtypeStruct((n, n), jnp.float32),
        in_specs=[pl.BlockSpec(memory_space=pltpu.VMEM)],
        out_specs=pl.BlockSpec(memory_space=pltpu.VMEM),
        scratch_shapes=[pltpu.VMEM((n, n), jnp.float32)],
        compiler_params=pltpu.CompilerParams(vmem_limit_bytes=VMEM_LIMIT),
    )(packed)


def sweep_call(packed, start_block, iters, scale):
    n, k = start_block.shape
    return pl.pallas_call(
        functools.partial(sweep_kernel, iters, scale),
        out_shape=jax.ShapeDtypeStruct((n, k), jnp.float32),
        in_specs=[pl.BlockSpec(memory_space=pltpu.VMEM)] * 2,
        out_specs=pl.BlockSpec(memory_space=pltpu.VMEM),
        scratch_shapes=[pltpu.VMEM((n, n), jnp.float32)],
        compiler_params=pltpu.CompilerParams(vmem_limit_bytes=VMEM_LIMIT),
    )(packed, start_block)


def modes(rows, subspace):
    return jnp.dot(
        rows.astype(jnp.float32), subspace, precision=lax.Precision.HIGHEST,
        preferred_element_type=jnp.float32,
    )


def tail_split(packed, start_block, iters, scale, rows):
    n, k = start_block.shape
    ndof = lax.axis_size("dof")
    core = lax.axis_index("dof") % 2
    to_odd = [(2 * i, 2 * i + 1) for i in range(ndof // 2)]
    to_even = [(2 * i + 1, 2 * i) for i in range(ndof // 2)]
    partner_rows = lax.ppermute(rows, "dof", to_odd)
    pod_shape = (rows.shape[0], k)

    def factor_side(p, b, own, other):
        zeros = jnp.zeros(pod_shape, jnp.float32)
        return chol_call(p, n, scale), zeros, zeros

    def sweep_side(p, b, own, other):
        blk = sweep_call(p, b, iters, scale)
        return jnp.zeros((n, n), jnp.float32), modes(own, blk), modes(other, blk)

    r_loc, pod_loc, pod_other = lax.cond(
        core == 0, factor_side, sweep_side, packed, start_block, rows, partner_rows)
    r_in = lax.ppermute(r_loc, "dof", to_odd)
    pod_in = lax.ppermute(pod_other, "dof", to_even)
    return r_loc + r_in, pod_loc + pod_in


STEPS = 64
ITERS = 3
PASSES = 16
TILE = 128


def pack_upper(rows):
    width = rows.shape[1]
    pieces = []
    for i in range(width // TILE):
        lhs = rows[:, i * TILE:(i + 1) * TILE]
        rhs = rows[:, i * TILE:]
        pieces.append(
            lax.dot_general(lhs, rhs, (((0,), (0,)), ((), ())), preferred_element_type=jnp.float32)
        )
    return jnp.concatenate(pieces, axis=1)


def all_reduce_a2a(x, axes):
    rows, cols = x.shape
    half = rows // 2
    ndof = lax.axis_size("dof")
    nsnap = lax.axis_size("snap")
    core = lax.axis_index("dof") % 2
    swap = [(i, i ^ 1) for i in range(ndof)]
    mine = lax.dynamic_slice_in_dim(x, core * half, half, 0)
    theirs = lax.dynamic_slice_in_dim(x, (1 - core) * half, half, 0)
    own = mine + lax.ppermute(theirs, "dof", swap)
    stacked = jnp.concatenate([own[:, :cols // 2], own[:, cols // 2:]], axis=0)
    received = lax.all_to_all(stacked, axes, 0, 0, tiled=True)
    by_core = received.reshape(ndof // 2, 2, nsnap, cols // 2).sum(axis=(0, 2))
    spread = jnp.broadcast_to(by_core[None, :, None, :], (ndof // 2, 2, nsnap, cols // 2))
    gathered = lax.all_to_all(spread.reshape(rows, cols // 2), axes, 0, 0, tiled=True)
    own_total = jnp.concatenate([gathered[:half], gathered[half:]], axis=1)
    other_total = lax.ppermute(own_total, "dof", swap)
    first = jnp.where(core == 0, own_total, other_total)
    second = jnp.where(core == 0, other_total, own_total)
    return jnp.concatenate([first, second], axis=0)


def body(snapshots, lengths, start_block):
    rows = lax.all_to_all(snapshots, "snap", 0, 1, tiled=True)
    width = rows.shape[1]
    col_length = jnp.repeat(lengths, STEPS, total_repeat_length=width)
    columns = jnp.arange(width, dtype=jnp.int32)
    active = columns % STEPS < col_length
    masked = jnp.where(active[None, :], rows, jnp.zeros_like(rows))
    row_count = snapshots.shape[0] * lax.axis_size("dof")
    packed = all_reduce_a2a(pack_upper(masked), ("dof", "snap"))
    upper_factor, pod_modes = tail_split(packed, start_block, ITERS, 1.0 / row_count, masked)
    return (pod_modes, upper_factor)


def solution(mesh):
    placed = (P("dof", "snap"), P(), P())
    return jax.shard_map(
        body, mesh=mesh, in_specs=placed, out_specs=(P(("dof", "snap"), None), P()), check_vma=False
    )
```

```python
import functools
import jax
import jax.numpy as jnp
from jax import lax
from jax.experimental import pallas as pl
from jax.experimental.pallas import tpu as pltpu
from jax.sharding import PartitionSpec as P


HI = lax.Precision.HIGHEST
LEAF = 128


def mm(a, b):
    return jnp.dot(a, b, precision=HI, preferred_element_type=jnp.float32)


def mm_tn(a, b):
    return lax.dot_general(a, b, (((0,), (0,)), ((), ())), precision=HI, preferred_element_type=jnp.float32)


def mm_nt(a, b):
    return lax.dot_general(a, b, (((1,), (1,)), ((), ())), precision=HI, preferred_element_type=jnp.float32)


def leaf_chol_inv(a):
    n = a.shape[0]
    row = lax.broadcasted_iota(jnp.int32, (n, 2 * n), 0)
    lane = lax.broadcasted_iota(jnp.int32, (n, 2 * n), 1)
    eye = jnp.where(row == lane - n, 1.0, 0.0).astype(jnp.float32)
    m0 = jnp.where(lane < n, jnp.concatenate([a, a], axis=1), eye)
    r2 = lax.broadcasted_iota(jnp.int32, (n, n), 0)
    c2 = lax.broadcasted_iota(jnp.int32, (n, n), 1)
    d0 = jnp.sum(jnp.where(r2 == c2, a, 0.0), axis=0, keepdims=True)
    row1 = lax.broadcasted_iota(jnp.int32, (n, 1), 0)
    lane1 = lax.broadcasted_iota(jnp.int32, (1, n), 1)

    def step(j, carry):
        m, d = carry
        pivot = jnp.sum(jnp.where(lane1 == j, d, 0.0), axis=1, keepdims=True)
        s = lax.rsqrt(pivot)
        pick_row = row == j
        prow = jnp.sum(jnp.where(pick_row, m, 0.0), axis=0, keepdims=True)
        col = jnp.sum(jnp.where(lane[:, :n] == j, m[:, :n], 0.0), axis=1, keepdims=True)
        nrow = prow * s
        mult = jnp.where(row1 > j, col * s, 0.0)
        head = nrow[:, :n]
        return jnp.where(pick_row, nrow, m - mult * nrow), d - head * head

    m, _ = lax.fori_loop(0, n, step, (m0, d0), unroll=4)
    u = jnp.where(r2 <= c2, m[:, :n], 0.0)
    w = m[:, n:]
    return u, w


def chol_inv(a, need_w):
    n = a.shape[0]
    if n <= LEAF:
        return leaf_chol_inv(a)
    h = n // 2
    u11, w11 = chol_inv(a[:h, :h], True)
    u12 = mm(w11, a[:h, h:])
    s = a[h:, h:] - mm_tn(u12, u12)
    u22, w22 = chol_inv(s, need_w)
    u = jnp.concatenate(
        [jnp.concatenate([u11, u12], axis=1),
         jnp.concatenate([jnp.zeros((h, h), jnp.float32), u22], axis=1)], axis=0)
    if not need_w:
        return u, None
    w21 = -mm(w22, mm_tn(u12, w11))
    w = jnp.concatenate(
        [jnp.concatenate([w11, jnp.zeros((h, h), jnp.float32)], axis=1),
         jnp.concatenate([w21, w22], axis=1)], axis=0)
    return u, w


def build_shifted(p_ref, sref, scale):
    n = sref.shape[0]
    eye = jnp.where(lax.broadcasted_iota(jnp.int32, (TILE, TILE), 0)
                    == lax.broadcasted_iota(jnp.int32, (TILE, TILE), 1), 0.05, 0.0).astype(jnp.float32)
    offset = 0
    for i in range(n // TILE):
        for j in range(i, n // TILE):
            c0 = offset + (j - i) * TILE
            blk = p_ref[:, c0:c0 + TILE] * scale
            if i == j:
                sref[i * TILE:(i + 1) * TILE, j * TILE:(j + 1) * TILE] = blk + eye
            else:
                sref[i * TILE:(i + 1) * TILE, j * TILE:(j + 1) * TILE] = blk
                sref[j * TILE:(j + 1) * TILE, i * TILE:(i + 1) * TILE] = jnp.transpose(blk)
        offset += n - i * TILE


def chol_kernel(scale, p_ref, r_ref, sref):
    build_shifted(p_ref, sref, scale)
    u, _ = chol_inv(sref[...], False)
    r_ref[...] = u


def sweep_kernel(iters, scale, p_ref, b_ref, out_ref, sref):
    build_shifted(p_ref, sref, scale)
    blk = b_ref[...]
    for _ in range(iters):
        image = mm(sref[...], blk)
        corr = mm_tn(image, image)
        _, w = chol_inv(corr, True)
        blk = mm_nt(image, w)
    out_ref[...] = blk


VMEM_LIMIT = 60 * 1024 * 1024


def chol_call(packed, n, scale):
    return pl.pallas_call(
        functools.partial(chol_kernel, scale),
        out_shape=jax.ShapeDtypeStruct((n, n), jnp.float32),
        in_specs=[pl.BlockSpec(memory_space=pltpu.VMEM)],
        out_specs=pl.BlockSpec(memory_space=pltpu.VMEM),
        scratch_shapes=[pltpu.VMEM((n, n), jnp.float32)],
        compiler_params=pltpu.CompilerParams(vmem_limit_bytes=VMEM_LIMIT),
    )(packed)


def sweep_call(packed, start_block, iters, scale):
    n, k = start_block.shape
    return pl.pallas_call(
        functools.partial(sweep_kernel, iters, scale),
        out_shape=jax.ShapeDtypeStruct((n, k), jnp.float32),
        in_specs=[pl.BlockSpec(memory_space=pltpu.VMEM)] * 2,
        out_specs=pl.BlockSpec(memory_space=pltpu.VMEM),
        scratch_shapes=[pltpu.VMEM((n, n), jnp.float32)],
        compiler_params=pltpu.CompilerParams(vmem_limit_bytes=VMEM_LIMIT),
    )(packed, start_block)


def tail_split(packed, start_block, iters, scale):
    n, k = start_block.shape
    core = lax.axis_index("dof") % 2

    def factor_side(a, b):
        return chol_call(a, n, scale), jnp.zeros((n, k), jnp.float32)

    def sweep_side(a, b):
        return jnp.zeros((n, n), jnp.float32), sweep_call(a, b, iters, scale)

    r_loc, b_loc = lax.cond(core == 0, factor_side, sweep_side, packed, start_block)
    pairs = lax.axis_size("dof") // 2
    r_in = lax.ppermute(r_loc, "dof", [(2 * i, 2 * i + 1) for i in range(pairs)])
    b_in = lax.ppermute(b_loc, "dof", [(2 * i + 1, 2 * i) for i in range(pairs)])
    return r_loc + r_in, b_loc + b_in


STEPS = 64
ITERS = 3
PASSES = 16
TILE = 128


def pack_upper(rows):
    width = rows.shape[1]
    pieces = []
    for i in range(width // TILE):
        lhs = rows[:, i * TILE:(i + 1) * TILE]
        rhs = rows[:, i * TILE:]
        pieces.append(
            lax.dot_general(lhs, rhs, (((0,), (0,)), ((), ())), preferred_element_type=jnp.float32)
        )
    return jnp.concatenate(pieces, axis=1)


def all_reduce_a2a(x, axes):
    rows, cols = x.shape
    half = rows // 2
    ndof = lax.axis_size("dof")
    nsnap = lax.axis_size("snap")
    core = lax.axis_index("dof") % 2
    swap = [(i, i ^ 1) for i in range(ndof)]
    mine = lax.dynamic_slice_in_dim(x, core * half, half, 0)
    theirs = lax.dynamic_slice_in_dim(x, (1 - core) * half, half, 0)
    own = mine + lax.ppermute(theirs, "dof", swap)
    stacked = jnp.concatenate([own[:, :cols // 2], own[:, cols // 2:]], axis=0)
    received = lax.all_to_all(stacked, axes, 0, 0, tiled=True)
    by_core = received.reshape(ndof // 2, 2, nsnap, cols // 2).sum(axis=(0, 2))
    spread = jnp.broadcast_to(by_core[None, :, None, :], (ndof // 2, 2, nsnap, cols // 2))
    gathered = lax.all_to_all(spread.reshape(rows, cols // 2), axes, 0, 0, tiled=True)
    own_total = jnp.concatenate([gathered[:half], gathered[half:]], axis=1)
    other_total = lax.ppermute(own_total, "dof", swap)
    first = jnp.where(core == 0, own_total, other_total)
    second = jnp.where(core == 0, other_total, own_total)
    return jnp.concatenate([first, second], axis=0)


def body(snapshots, lengths, start_block):
    rows = lax.all_to_all(snapshots, "snap", 0, 1, tiled=True)
    width = rows.shape[1]
    col_length = jnp.repeat(lengths, STEPS, total_repeat_length=width)
    columns = jnp.arange(width, dtype=jnp.int32)
    active = columns % STEPS < col_length
    masked = jnp.where(active[None, :], rows, jnp.zeros_like(rows))
    row_count = snapshots.shape[0] * lax.axis_size("dof")
    packed = all_reduce_a2a(pack_upper(masked), ("dof", "snap"))
    upper_factor, subspace = tail_split(packed, start_block, ITERS, 1.0 / row_count)
    pod_modes = jnp.dot(
        masked.astype(jnp.float32), subspace, precision=lax.Precision.HIGHEST,
        preferred_element_type=jnp.float32,
    )
    return (pod_modes, upper_factor)


def solution(mesh):
    placed = (P("dof", "snap"), P(), P())
    return jax.shard_map(
        body, mesh=mesh, in_specs=placed, out_specs=(P(("dof", "snap"), None), P()), check_vma=False
    )
```

```python
import functools
import jax
import jax.numpy as jnp
from jax import lax
from jax.experimental import pallas as pl
from jax.experimental.pallas import tpu as pltpu
from jax.sharding import PartitionSpec as P


HI = lax.Precision.HIGHEST
LEAF = 128


def mm(a, b):
    return jnp.dot(a, b, precision=HI, preferred_element_type=jnp.float32)


def mm_tn(a, b):
    return lax.dot_general(a, b, (((0,), (0,)), ((), ())), precision=HI, preferred_element_type=jnp.float32)


def mm_nt(a, b):
    return lax.dot_general(a, b, (((1,), (1,)), ((), ())), precision=HI, preferred_element_type=jnp.float32)


def leaf_chol_inv(a):
    n = a.shape[0]
    row = lax.broadcasted_iota(jnp.int32, (n, 2 * n), 0)
    lane = lax.broadcasted_iota(jnp.int32, (n, 2 * n), 1)
    eye = jnp.where(row == lane - n, 1.0, 0.0).astype(jnp.float32)
    m0 = jnp.where(lane < n, jnp.concatenate([a, a], axis=1), eye)
    r2 = lax.broadcasted_iota(jnp.int32, (n, n), 0)
    c2 = lax.broadcasted_iota(jnp.int32, (n, n), 1)
    d0 = jnp.sum(jnp.where(r2 == c2, a, 0.0), axis=0, keepdims=True)
    row1 = lax.broadcasted_iota(jnp.int32, (n, 1), 0)
    lane1 = lax.broadcasted_iota(jnp.int32, (1, n), 1)

    def step(j, carry):
        m, d = carry
        pivot = jnp.sum(jnp.where(lane1 == j, d, 0.0), axis=1, keepdims=True)
        s = lax.rsqrt(pivot)
        pick_row = row == j
        prow = jnp.sum(jnp.where(pick_row, m, 0.0), axis=0, keepdims=True)
        col = jnp.sum(jnp.where(lane[:, :n] == j, m[:, :n], 0.0), axis=1, keepdims=True)
        nrow = prow * s
        mult = jnp.where(row1 > j, col * s, 0.0)
        head = nrow[:, :n]
        return jnp.where(pick_row, nrow, m - mult * nrow), d - head * head

    m, _ = lax.fori_loop(0, n, step, (m0, d0), unroll=4)
    u = jnp.where(r2 <= c2, m[:, :n], 0.0)
    w = m[:, n:]
    return u, w


def chol_inv(a, need_w):
    n = a.shape[0]
    if n <= LEAF:
        return leaf_chol_inv(a)
    h = n // 2
    u11, w11 = chol_inv(a[:h, :h], True)
    u12 = mm(w11, a[:h, h:])
    s = a[h:, h:] - mm_tn(u12, u12)
    u22, w22 = chol_inv(s, need_w)
    u = jnp.concatenate(
        [jnp.concatenate([u11, u12], axis=1),
         jnp.concatenate([jnp.zeros((h, h), jnp.float32), u22], axis=1)], axis=0)
    if not need_w:
        return u, None
    w21 = -mm(w22, mm_tn(u12, w11))
    w = jnp.concatenate(
        [jnp.concatenate([w11, jnp.zeros((h, h), jnp.float32)], axis=1),
         jnp.concatenate([w21, w22], axis=1)], axis=0)
    return u, w


def build_shifted(p_ref, sref, scale):
    n = sref.shape[0]
    eye = jnp.where(lax.broadcasted_iota(jnp.int32, (TILE, TILE), 0)
                    == lax.broadcasted_iota(jnp.int32, (TILE, TILE), 1), 0.05, 0.0).astype(jnp.float32)
    offset = 0
    for i in range(n // TILE):
        for j in range(i, n // TILE):
            c0 = offset + (j - i) * TILE
            blk = p_ref[:, c0:c0 + TILE] * scale
            if i == j:
                sref[i * TILE:(i + 1) * TILE, j * TILE:(j + 1) * TILE] = blk + eye
            else:
                sref[i * TILE:(i + 1) * TILE, j * TILE:(j + 1) * TILE] = blk
                sref[j * TILE:(j + 1) * TILE, i * TILE:(i + 1) * TILE] = jnp.transpose(blk)
        offset += n - i * TILE


def chol_kernel(scale, p_ref, r_ref, sref):
    build_shifted(p_ref, sref, scale)
    u, _ = chol_inv(sref[...], False)
    r_ref[...] = u


def sweep_kernel(iters, scale, p_ref, b_ref, out_ref, sref):
    build_shifted(p_ref, sref, scale)
    blk = b_ref[...]
    for _ in range(iters):
        image = mm(sref[...], blk)
        corr = mm_tn(image, image)
        _, w = chol_inv(corr, True)
        blk = mm_nt(image, w)
    out_ref[...] = blk


VMEM_LIMIT = 60 * 1024 * 1024


def chol_call(packed, n, scale):
    return pl.pallas_call(
        functools.partial(chol_kernel, scale),
        out_shape=jax.ShapeDtypeStruct((n, n), jnp.float32),
        in_specs=[pl.BlockSpec(memory_space=pltpu.VMEM)],
        out_specs=pl.BlockSpec(memory_space=pltpu.VMEM),
        scratch_shapes=[pltpu.VMEM((n, n), jnp.float32)],
        compiler_params=pltpu.CompilerParams(vmem_limit_bytes=VMEM_LIMIT),
    )(packed)


def sweep_call(packed, start_block, iters, scale):
    n, k = start_block.shape
    return pl.pallas_call(
        functools.partial(sweep_kernel, iters, scale),
        out_shape=jax.ShapeDtypeStruct((n, k), jnp.float32),
        in_specs=[pl.BlockSpec(memory_space=pltpu.VMEM)] * 2,
        out_specs=pl.BlockSpec(memory_space=pltpu.VMEM),
        scratch_shapes=[pltpu.VMEM((n, n), jnp.float32)],
        compiler_params=pltpu.CompilerParams(vmem_limit_bytes=VMEM_LIMIT),
    )(packed, start_block)


def tail_split(packed, start_block, iters, scale):
    n, k = start_block.shape
    core = lax.axis_index("dof") % 2

    def factor_side(a, b):
        return chol_call(a, n, scale), jnp.zeros((n, k), jnp.float32)

    def sweep_side(a, b):
        return jnp.zeros((n, n), jnp.float32), sweep_call(a, b, iters, scale)

    r_loc, b_loc = lax.cond(core == 0, factor_side, sweep_side, packed, start_block)
    pairs = lax.axis_size("dof") // 2
    r_in = lax.ppermute(r_loc, "dof", [(2 * i, 2 * i + 1) for i in range(pairs)])
    b_in = lax.ppermute(b_loc, "dof", [(2 * i + 1, 2 * i) for i in range(pairs)])
    r_out = lax.cond(core == 0, lambda a, b: a, lambda a, b: b, r_loc, r_in)
    return r_out, b_loc + b_in


STEPS = 64
ITERS = 3
PASSES = 16
TILE = 128


def pack_upper(rows):
    width = rows.shape[1]
    pieces = []
    for i in range(width // TILE):
        lhs = rows[:, i * TILE:(i + 1) * TILE]
        rhs = rows[:, i * TILE:]
        pieces.append(
            lax.dot_general(lhs, rhs, (((0,), (0,)), ((), ())), preferred_element_type=jnp.float32)
        )
    return jnp.concatenate(pieces, axis=1)


def all_reduce_a2a(x, axes):
    rows, cols = x.shape
    half = rows // 2
    ndof = lax.axis_size("dof")
    nsnap = lax.axis_size("snap")
    core = lax.axis_index("dof") % 2
    swap = [(i, i ^ 1) for i in range(ndof)]
    mine = lax.dynamic_slice_in_dim(x, core * half, half, 0)
    theirs = lax.dynamic_slice_in_dim(x, (1 - core) * half, half, 0)
    own = mine + lax.ppermute(theirs, "dof", swap)
    stacked = jnp.concatenate([own[:, :cols // 2], own[:, cols // 2:]], axis=0)
    received = lax.all_to_all(stacked, axes, 0, 0, tiled=True)
    by_core = received.reshape(ndof // 2, 2, nsnap, cols // 2).sum(axis=(0, 2))
    spread = jnp.broadcast_to(by_core[None, :, None, :], (ndof // 2, 2, nsnap, cols // 2))
    gathered = lax.all_to_all(spread.reshape(rows, cols // 2), axes, 0, 0, tiled=True)
    own_total = jnp.concatenate([gathered[:half], gathered[half:]], axis=1)
    other_total = lax.ppermute(own_total, "dof", swap)
    first = jnp.where(core == 0, own_total, other_total)
    second = jnp.where(core == 0, other_total, own_total)
    return jnp.concatenate([first, second], axis=0)


def body(snapshots, lengths, start_block):
    rows = lax.all_to_all(snapshots, "snap", 0, 1, tiled=True)
    width = rows.shape[1]
    col_length = jnp.repeat(lengths, STEPS, total_repeat_length=width)
    columns = jnp.arange(width, dtype=jnp.int32)
    active = columns % STEPS < col_length
    masked = jnp.where(active[None, :], rows, jnp.zeros_like(rows))
    row_count = snapshots.shape[0] * lax.axis_size("dof")
    packed = all_reduce_a2a(pack_upper(masked), ("dof", "snap"))
    upper_factor, subspace = tail_split(packed, start_block, ITERS, 1.0 / row_count)
    hi32 = lax.reduce_precision(subspace, exponent_bits=8, mantissa_bits=7)
    rest = subspace - hi32
    mid32 = lax.reduce_precision(rest, exponent_bits=8, mantissa_bits=7)
    lo32 = lax.reduce_precision(rest - mid32, exponent_bits=8, mantissa_bits=7)
    hi, mid, lo = (p.astype(jnp.bfloat16) for p in (hi32, mid32, lo32))
    pod_modes = sum(
        jnp.dot(masked, part, preferred_element_type=jnp.float32) for part in (hi, mid, lo)
    )
    return (pod_modes, upper_factor)


def solution(mesh):
    placed = (P("dof", "snap"), P(), P())
    return jax.shard_map(
        body, mesh=mesh, in_specs=placed, out_specs=(P(("dof", "snap"), None), P()), check_vma=False
    )
```

```python
import functools
import jax
import jax.numpy as jnp
from jax import lax
from jax.experimental import pallas as pl
from jax.experimental.pallas import tpu as pltpu
from jax.sharding import PartitionSpec as P


HI = lax.Precision.HIGHEST
LEAF = 128


def mm(a, b):
    return jnp.dot(a, b, precision=HI, preferred_element_type=jnp.float32)


def mm_tn(a, b):
    return lax.dot_general(a, b, (((0,), (0,)), ((), ())), precision=HI, preferred_element_type=jnp.float32)


def mm_nt(a, b):
    return lax.dot_general(a, b, (((1,), (1,)), ((), ())), precision=HI, preferred_element_type=jnp.float32)


def leaf_chol_inv(a):
    n = a.shape[0]
    row = lax.broadcasted_iota(jnp.int32, (n, 2 * n), 0)
    lane = lax.broadcasted_iota(jnp.int32, (n, 2 * n), 1)
    eye = jnp.where(row == lane - n, 1.0, 0.0).astype(jnp.float32)
    m0 = jnp.where(lane < n, jnp.concatenate([a, a], axis=1), eye)
    r2 = lax.broadcasted_iota(jnp.int32, (n, n), 0)
    c2 = lax.broadcasted_iota(jnp.int32, (n, n), 1)
    d0 = jnp.sum(jnp.where(r2 == c2, a, 0.0), axis=0, keepdims=True)
    row1 = lax.broadcasted_iota(jnp.int32, (n, 1), 0)
    lane1 = lax.broadcasted_iota(jnp.int32, (1, n), 1)

    def step(j, carry):
        m, d = carry
        pivot = jnp.sum(jnp.where(lane1 == j, d, 0.0), axis=1, keepdims=True)
        s = lax.rsqrt(pivot)
        pick_row = row == j
        prow = jnp.sum(jnp.where(pick_row, m, 0.0), axis=0, keepdims=True)
        col = jnp.sum(jnp.where(lane[:, :n] == j, m[:, :n], 0.0), axis=1, keepdims=True)
        nrow = prow * s
        mult = jnp.where(row1 > j, col * s, 0.0)
        head = nrow[:, :n]
        return jnp.where(pick_row, nrow, m - mult * nrow), d - head * head

    m, _ = lax.fori_loop(0, n, step, (m0, d0), unroll=4)
    u = jnp.where(r2 <= c2, m[:, :n], 0.0)
    w = m[:, n:]
    return u, w


def chol_inv(a, need_w):
    n = a.shape[0]
    if n <= LEAF:
        return leaf_chol_inv(a)
    h = n // 2
    u11, w11 = chol_inv(a[:h, :h], True)
    u12 = mm(w11, a[:h, h:])
    s = a[h:, h:] - mm_tn(u12, u12)
    u22, w22 = chol_inv(s, need_w)
    u = jnp.concatenate(
        [jnp.concatenate([u11, u12], axis=1),
         jnp.concatenate([jnp.zeros((h, h), jnp.float32), u22], axis=1)], axis=0)
    if not need_w:
        return u, None
    w21 = -mm(w22, mm_tn(u12, w11))
    w = jnp.concatenate(
        [jnp.concatenate([w11, jnp.zeros((h, h), jnp.float32)], axis=1),
         jnp.concatenate([w21, w22], axis=1)], axis=0)
    return u, w


def build_shifted(p_ref, sref, scale):
    n = sref.shape[0]
    eye = jnp.where(lax.broadcasted_iota(jnp.int32, (TILE, TILE), 0)
                    == lax.broadcasted_iota(jnp.int32, (TILE, TILE), 1), 0.05, 0.0).astype(jnp.float32)
    offset = 0
    for i in range(n // TILE):
        for j in range(i, n // TILE):
            c0 = offset + (j - i) * TILE
            blk = p_ref[:, c0:c0 + TILE] * scale
            if i == j:
                sref[i * TILE:(i + 1) * TILE, j * TILE:(j + 1) * TILE] = blk + eye
            else:
                sref[i * TILE:(i + 1) * TILE, j * TILE:(j + 1) * TILE] = blk
                sref[j * TILE:(j + 1) * TILE, i * TILE:(i + 1) * TILE] = jnp.transpose(blk)
        offset += n - i * TILE


def chol_kernel(scale, p_ref, r_ref, sref):
    build_shifted(p_ref, sref, scale)
    u, _ = chol_inv(sref[...], False)
    r_ref[...] = u


def sweep_kernel(iters, scale, p_ref, b_ref, out_ref, sref):
    build_shifted(p_ref, sref, scale)
    blk = b_ref[...]
    for _ in range(iters):
        image = mm(sref[...], blk)
        corr = mm_tn(image, image)
        _, w = chol_inv(corr, True)
        blk = mm_nt(image, w)
    out_ref[...] = blk


VMEM_LIMIT = 60 * 1024 * 1024


def chol_call(packed, n, scale):
    return pl.pallas_call(
        functools.partial(chol_kernel, scale),
        out_shape=jax.ShapeDtypeStruct((n, n), jnp.float32),
        in_specs=[pl.BlockSpec(memory_space=pltpu.VMEM)],
        out_specs=pl.BlockSpec(memory_space=pltpu.VMEM),
        scratch_shapes=[pltpu.VMEM((n, n), jnp.float32)],
        compiler_params=pltpu.CompilerParams(vmem_limit_bytes=VMEM_LIMIT),
    )(packed)


def sweep_call(packed, start_block, iters, scale):
    n, k = start_block.shape
    return pl.pallas_call(
        functools.partial(sweep_kernel, iters, scale),
        out_shape=jax.ShapeDtypeStruct((n, k), jnp.float32),
        in_specs=[pl.BlockSpec(memory_space=pltpu.VMEM)] * 2,
        out_specs=pl.BlockSpec(memory_space=pltpu.VMEM),
        scratch_shapes=[pltpu.VMEM((n, n), jnp.float32)],
        compiler_params=pltpu.CompilerParams(vmem_limit_bytes=VMEM_LIMIT),
    )(packed, start_block)


def tail_split(packed, start_block, iters, scale):
    n, k = start_block.shape
    core = lax.axis_index("dof") % 2

    def factor_side(a, b):
        return chol_call(a, n, scale), jnp.zeros((n, k), jnp.float32)

    def sweep_side(a, b):
        return jnp.zeros((n, n), jnp.float32), sweep_call(a, b, iters, scale)

    r_loc, b_loc = lax.cond(core == 0, factor_side, sweep_side, packed, start_block)
    pairs = lax.axis_size("dof") // 2
    r_in = lax.ppermute(r_loc, "dof", [(2 * i, 2 * i + 1) for i in range(pairs)])
    b_in = lax.ppermute(b_loc, "dof", [(2 * i + 1, 2 * i) for i in range(pairs)])
    return r_loc + r_in, b_loc + b_in


STEPS = 64
ITERS = 3
PASSES = 16
TILE = 128


def pack_upper(rows):
    width = rows.shape[1]
    pieces = []
    for i in range(width // TILE):
        lhs = rows[:, i * TILE:(i + 1) * TILE]
        rhs = rows[:, i * TILE:]
        pieces.append(
            lax.dot_general(lhs, rhs, (((0,), (0,)), ((), ())), preferred_element_type=jnp.float32)
        )
    return jnp.concatenate(pieces, axis=1)


def all_reduce_a2a(x, axes):
    rows, cols = x.shape
    half = rows // 2
    ndof = lax.axis_size("dof")
    nsnap = lax.axis_size("snap")
    core = lax.axis_index("dof") % 2
    swap = [(i, i ^ 1) for i in range(ndof)]
    mine = lax.dynamic_slice_in_dim(x, core * half, half, 0)
    theirs = lax.dynamic_slice_in_dim(x, (1 - core) * half, half, 0)
    own = mine + lax.ppermute(theirs, "dof", swap)
    stacked = jnp.concatenate([own[:, :cols // 2], own[:, cols // 2:]], axis=0)
    received = lax.all_to_all(stacked, axes, 0, 0, tiled=True)
    by_core = received.reshape(ndof // 2, 2, nsnap, cols // 2).sum(axis=(0, 2))
    spread = jnp.broadcast_to(by_core[None, :, None, :], (ndof // 2, 2, nsnap, cols // 2))
    gathered = lax.all_to_all(spread.reshape(rows, cols // 2), axes, 0, 0, tiled=True)
    own_total = jnp.concatenate([gathered[:half], gathered[half:]], axis=1)
    other_total = lax.ppermute(own_total, "dof", swap)
    first = jnp.where(core == 0, own_total, other_total)
    second = jnp.where(core == 0, other_total, own_total)
    return jnp.concatenate([first, second], axis=0)


def body(snapshots, lengths, start_block):
    rows = lax.all_to_all(snapshots, "snap", 0, 1, tiled=True)
    width = rows.shape[1]
    col_length = jnp.repeat(lengths, STEPS, total_repeat_length=width)
    columns = jnp.arange(width, dtype=jnp.int32)
    active = columns % STEPS < col_length
    masked = jnp.where(active[None, :], rows, jnp.zeros_like(rows))
    row_count = snapshots.shape[0] * lax.axis_size("dof")
    packed = all_reduce_a2a(pack_upper(masked), ("dof", "snap"))
    upper_factor, subspace = tail_split(packed, start_block, ITERS, 1.0 / row_count)
    hi32 = lax.reduce_precision(subspace, exponent_bits=8, mantissa_bits=7)
    rest = subspace - hi32
    mid32 = lax.reduce_precision(rest, exponent_bits=8, mantissa_bits=7)
    lo32 = lax.reduce_precision(rest - mid32, exponent_bits=8, mantissa_bits=7)
    hi, mid, lo = (p.astype(jnp.bfloat16) for p in (hi32, mid32, lo32))
    pod_modes = sum(
        jnp.dot(masked, part, preferred_element_type=jnp.float32) for part in (hi, mid, lo)
    )
    return (pod_modes, upper_factor)


def solution(mesh):
    placed = (P("dof", "snap"), P(), P())
    return jax.shard_map(
        body, mesh=mesh, in_specs=placed, out_specs=(P(("dof", "snap"), None), P()), check_vma=False
    )
```

```python
import functools
import jax
import jax.numpy as jnp
from jax import lax
from jax.experimental import pallas as pl
from jax.experimental.pallas import tpu as pltpu
from jax.sharding import PartitionSpec as P


HI = lax.Precision.HIGHEST
MID = lax.Precision.HIGH
LEAF = 128


def mm(a, b, precision=HI):
    return jnp.dot(a, b, precision=precision, preferred_element_type=jnp.float32)


def mm_tn(a, b, precision=HI):
    return lax.dot_general(a, b, (((0,), (0,)), ((), ())), precision=precision, preferred_element_type=jnp.float32)


def mm_nt(a, b):
    return lax.dot_general(a, b, (((1,), (1,)), ((), ())), precision=HI, preferred_element_type=jnp.float32)


def leaf_chol_inv(a):
    n = a.shape[0]
    row = lax.broadcasted_iota(jnp.int32, (n, 2 * n), 0)
    lane = lax.broadcasted_iota(jnp.int32, (n, 2 * n), 1)
    eye = jnp.where(row == lane - n, 1.0, 0.0).astype(jnp.float32)
    m0 = jnp.where(lane < n, jnp.concatenate([a, a], axis=1), eye)
    r2 = lax.broadcasted_iota(jnp.int32, (n, n), 0)
    c2 = lax.broadcasted_iota(jnp.int32, (n, n), 1)
    d0 = jnp.sum(jnp.where(r2 == c2, a, 0.0), axis=0, keepdims=True)
    row1 = lax.broadcasted_iota(jnp.int32, (n, 1), 0)
    lane1 = lax.broadcasted_iota(jnp.int32, (1, n), 1)

    def step(j, carry):
        m, d = carry
        pivot = jnp.sum(jnp.where(lane1 == j, d, 0.0), axis=1, keepdims=True)
        s = lax.rsqrt(pivot)
        pick_row = row == j
        prow = jnp.sum(jnp.where(pick_row, m, 0.0), axis=0, keepdims=True)
        col = jnp.sum(jnp.where(lane[:, :n] == j, m[:, :n], 0.0), axis=1, keepdims=True)
        nrow = prow * s
        mult = jnp.where(row1 > j, col * s, 0.0)
        head = nrow[:, :n]
        return jnp.where(pick_row, nrow, m - mult * nrow), d - head * head

    m, _ = lax.fori_loop(0, n, step, (m0, d0), unroll=4)
    u = jnp.where(r2 <= c2, m[:, :n], 0.0)
    w = m[:, n:]
    return u, w


def chol_inv(a, need_w):
    n = a.shape[0]
    if n <= LEAF:
        return leaf_chol_inv(a)
    h = n // 2
    u11, w11 = chol_inv(a[:h, :h], True)
    u12 = mm(w11, a[:h, h:], MID)
    s = a[h:, h:] - mm_tn(u12, u12, MID)
    u22, w22 = chol_inv(s, need_w)
    u = jnp.concatenate(
        [jnp.concatenate([u11, u12], axis=1),
         jnp.concatenate([jnp.zeros((h, h), jnp.float32), u22], axis=1)], axis=0)
    if not need_w:
        return u, None
    w21 = -mm(w22, mm_tn(u12, w11, MID), MID)
    w = jnp.concatenate(
        [jnp.concatenate([w11, jnp.zeros((h, h), jnp.float32)], axis=1),
         jnp.concatenate([w21, w22], axis=1)], axis=0)
    return u, w


def build_shifted(p_ref, sref, scale):
    n = sref.shape[0]
    eye = jnp.where(lax.broadcasted_iota(jnp.int32, (TILE, TILE), 0)
                    == lax.broadcasted_iota(jnp.int32, (TILE, TILE), 1), 0.05, 0.0).astype(jnp.float32)
    offset = 0
    for i in range(n // TILE):
        for j in range(i, n // TILE):
            c0 = offset + (j - i) * TILE
            blk = p_ref[:, c0:c0 + TILE] * scale
            if i == j:
                sref[i * TILE:(i + 1) * TILE, j * TILE:(j + 1) * TILE] = blk + eye
            else:
                sref[i * TILE:(i + 1) * TILE, j * TILE:(j + 1) * TILE] = blk
                sref[j * TILE:(j + 1) * TILE, i * TILE:(i + 1) * TILE] = jnp.transpose(blk)
        offset += n - i * TILE


def chol_kernel(scale, p_ref, r_ref, sref):
    build_shifted(p_ref, sref, scale)
    u, _ = chol_inv(sref[...], False)
    r_ref[...] = u


def sweep_kernel(iters, scale, p_ref, b_ref, out_ref, sref):
    build_shifted(p_ref, sref, scale)
    blk = b_ref[...]
    for _ in range(iters):
        image = mm(sref[...], blk)
        corr = mm_tn(image, image)
        _, w = chol_inv(corr, True)
        blk = mm_nt(image, w)
    out_ref[...] = blk


VMEM_LIMIT = 60 * 1024 * 1024


def chol_call(packed, n, scale):
    return pl.pallas_call(
        functools.partial(chol_kernel, scale),
        out_shape=jax.ShapeDtypeStruct((n, n), jnp.float32),
        in_specs=[pl.BlockSpec(memory_space=pltpu.VMEM)],
        out_specs=pl.BlockSpec(memory_space=pltpu.VMEM),
        scratch_shapes=[pltpu.VMEM((n, n), jnp.float32)],
        compiler_params=pltpu.CompilerParams(vmem_limit_bytes=VMEM_LIMIT),
    )(packed)


def sweep_call(packed, start_block, iters, scale):
    n, k = start_block.shape
    return pl.pallas_call(
        functools.partial(sweep_kernel, iters, scale),
        out_shape=jax.ShapeDtypeStruct((n, k), jnp.float32),
        in_specs=[pl.BlockSpec(memory_space=pltpu.VMEM)] * 2,
        out_specs=pl.BlockSpec(memory_space=pltpu.VMEM),
        scratch_shapes=[pltpu.VMEM((n, n), jnp.float32)],
        compiler_params=pltpu.CompilerParams(vmem_limit_bytes=VMEM_LIMIT),
    )(packed, start_block)


def tail_split(packed, start_block, iters, scale):
    n, k = start_block.shape
    core = lax.axis_index("dof") % 2

    def factor_side(a, b):
        return chol_call(a, n, scale), jnp.zeros((n, k), jnp.float32)

    def sweep_side(a, b):
        return jnp.zeros((n, n), jnp.float32), sweep_call(a, b, iters, scale)

    r_loc, b_loc = lax.cond(core == 0, factor_side, sweep_side, packed, start_block)
    pairs = lax.axis_size("dof") // 2
    r_in = lax.ppermute(r_loc, "dof", [(2 * i, 2 * i + 1) for i in range(pairs)])
    b_in = lax.ppermute(b_loc, "dof", [(2 * i + 1, 2 * i) for i in range(pairs)])
    return r_loc + r_in, b_loc + b_in


STEPS = 64
ITERS = 3
PASSES = 16
TILE = 128


def pack_upper(rows):
    width = rows.shape[1]
    pieces = []
    for i in range(width // TILE):
        lhs = rows[:, i * TILE:(i + 1) * TILE]
        rhs = rows[:, i * TILE:]
        pieces.append(
            lax.dot_general(lhs, rhs, (((0,), (0,)), ((), ())), preferred_element_type=jnp.float32)
        )
    return jnp.concatenate(pieces, axis=1)


def all_reduce_a2a(x, axes):
    rows, cols = x.shape
    half = rows // 2
    ndof = lax.axis_size("dof")
    nsnap = lax.axis_size("snap")
    core = lax.axis_index("dof") % 2
    swap = [(i, i ^ 1) for i in range(ndof)]
    mine = lax.dynamic_slice_in_dim(x, core * half, half, 0)
    theirs = lax.dynamic_slice_in_dim(x, (1 - core) * half, half, 0)
    own = mine + lax.ppermute(theirs, "dof", swap)
    stacked = jnp.concatenate([own[:, :cols // 2], own[:, cols // 2:]], axis=0)
    received = lax.all_to_all(stacked, axes, 0, 0, tiled=True)
    by_core = received.reshape(ndof // 2, 2, nsnap, cols // 2).sum(axis=(0, 2))
    spread = jnp.broadcast_to(by_core[None, :, None, :], (ndof // 2, 2, nsnap, cols // 2))
    gathered = lax.all_to_all(spread.reshape(rows, cols // 2), axes, 0, 0, tiled=True)
    own_total = jnp.concatenate([gathered[:half], gathered[half:]], axis=1)
    other_total = lax.ppermute(own_total, "dof", swap)
    first = jnp.where(core == 0, own_total, other_total)
    second = jnp.where(core == 0, other_total, own_total)
    return jnp.concatenate([first, second], axis=0)


def body(snapshots, lengths, start_block):
    rows = lax.all_to_all(snapshots, "snap", 0, 1, tiled=True)
    width = rows.shape[1]
    col_length = jnp.repeat(lengths, STEPS, total_repeat_length=width)
    columns = jnp.arange(width, dtype=jnp.int32)
    active = columns % STEPS < col_length
    masked = jnp.where(active[None, :], rows, jnp.zeros_like(rows))
    row_count = snapshots.shape[0] * lax.axis_size("dof")
    packed = all_reduce_a2a(pack_upper(masked), ("dof", "snap"))
    upper_factor, subspace = tail_split(packed, start_block, ITERS, 1.0 / row_count)
    pod_modes = jnp.dot(
        masked.astype(jnp.float32), subspace, precision=lax.Precision.HIGHEST,
        preferred_element_type=jnp.float32,
    )
    return (pod_modes, upper_factor)


def solution(mesh):
    placed = (P("dof", "snap"), P(), P())
    return jax.shard_map(
        body, mesh=mesh, in_specs=placed, out_specs=(P(("dof", "snap"), None), P()), check_vma=False
    )
```

```python
import functools
import jax
import jax.numpy as jnp
from jax import lax
from jax.experimental import pallas as pl
from jax.experimental.pallas import tpu as pltpu
from jax.sharding import PartitionSpec as P


HI = lax.Precision.HIGHEST
MID = lax.Precision.HIGH
LEAF = 128


def mm(a, b, precision=HI):
    return jnp.dot(a, b, precision=precision, preferred_element_type=jnp.float32)


def mm_tn(a, b, precision=HI):
    return lax.dot_general(a, b, (((0,), (0,)), ((), ())), precision=precision, preferred_element_type=jnp.float32)


def mm_nt(a, b):
    return lax.dot_general(a, b, (((1,), (1,)), ((), ())), precision=HI, preferred_element_type=jnp.float32)


def leaf_chol_inv(a, unroll):
    n = a.shape[0]
    row = lax.broadcasted_iota(jnp.int32, (n, 2 * n), 0)
    lane = lax.broadcasted_iota(jnp.int32, (n, 2 * n), 1)
    eye = jnp.where(row == lane - n, 1.0, 0.0).astype(jnp.float32)
    m0 = jnp.where(lane < n, jnp.concatenate([a, a], axis=1), eye)
    r2 = lax.broadcasted_iota(jnp.int32, (n, n), 0)
    c2 = lax.broadcasted_iota(jnp.int32, (n, n), 1)
    d0 = jnp.sum(jnp.where(r2 == c2, a, 0.0), axis=0, keepdims=True)
    row1 = lax.broadcasted_iota(jnp.int32, (n, 1), 0)
    lane1 = lax.broadcasted_iota(jnp.int32, (1, n), 1)

    def step(j, carry):
        m, d = carry
        pivot = jnp.sum(jnp.where(lane1 == j, d, 0.0), axis=1, keepdims=True)
        s = lax.rsqrt(pivot)
        pick_row = row == j
        prow = jnp.sum(jnp.where(pick_row, m, 0.0), axis=0, keepdims=True)
        col = jnp.sum(jnp.where(lane[:, :n] == j, m[:, :n], 0.0), axis=1, keepdims=True)
        nrow = prow * s
        mult = jnp.where(row1 > j, col * s, 0.0)
        head = nrow[:, :n]
        return jnp.where(pick_row, nrow, m - mult * nrow), d - head * head

    m, _ = lax.fori_loop(0, n, step, (m0, d0), unroll=unroll)
    u = jnp.where(r2 <= c2, m[:, :n], 0.0)
    w = m[:, n:]
    return u, w


def chol_inv(a, need_w, unroll=4):
    n = a.shape[0]
    if n <= LEAF:
        return leaf_chol_inv(a, unroll)
    h = n // 2
    u11, w11 = chol_inv(a[:h, :h], True)
    u12 = mm(w11, a[:h, h:], MID)
    s = a[h:, h:] - mm_tn(u12, u12, MID)
    u22, w22 = chol_inv(s, need_w)
    u = jnp.concatenate(
        [jnp.concatenate([u11, u12], axis=1),
         jnp.concatenate([jnp.zeros((h, h), jnp.float32), u22], axis=1)], axis=0)
    if not need_w:
        return u, None
    w21 = -mm(w22, mm_tn(u12, w11, MID), MID)
    w = jnp.concatenate(
        [jnp.concatenate([w11, jnp.zeros((h, h), jnp.float32)], axis=1),
         jnp.concatenate([w21, w22], axis=1)], axis=0)
    return u, w


def build_shifted(p_ref, sref, scale):
    n = sref.shape[0]
    eye = jnp.where(lax.broadcasted_iota(jnp.int32, (TILE, TILE), 0)
                    == lax.broadcasted_iota(jnp.int32, (TILE, TILE), 1), 0.05, 0.0).astype(jnp.float32)
    offset = 0
    for i in range(n // TILE):
        for j in range(i, n // TILE):
            c0 = offset + (j - i) * TILE
            blk = p_ref[:, c0:c0 + TILE] * scale
            if i == j:
                sref[i * TILE:(i + 1) * TILE, j * TILE:(j + 1) * TILE] = blk + eye
            else:
                sref[i * TILE:(i + 1) * TILE, j * TILE:(j + 1) * TILE] = blk
                sref[j * TILE:(j + 1) * TILE, i * TILE:(i + 1) * TILE] = jnp.transpose(blk)
        offset += n - i * TILE


def chol_kernel(scale, p_ref, r_ref, sref):
    build_shifted(p_ref, sref, scale)
    u, _ = chol_inv(sref[...], False)
    r_ref[...] = u


def sweep_kernel(iters, scale, p_ref, b_ref, out_ref, sref):
    build_shifted(p_ref, sref, scale)
    blk = b_ref[...]
    for _ in range(iters):
        image = mm(sref[...], blk)
        corr = mm_tn(image, image)
        _, w = chol_inv(corr, True, unroll=1)
        blk = mm_nt(image, w)
    out_ref[...] = blk


VMEM_LIMIT = 60 * 1024 * 1024


def chol_call(packed, n, scale):
    return pl.pallas_call(
        functools.partial(chol_kernel, scale),
        out_shape=jax.ShapeDtypeStruct((n, n), jnp.float32),
        in_specs=[pl.BlockSpec(memory_space=pltpu.VMEM)],
        out_specs=pl.BlockSpec(memory_space=pltpu.VMEM),
        scratch_shapes=[pltpu.VMEM((n, n), jnp.float32)],
        compiler_params=pltpu.CompilerParams(vmem_limit_bytes=VMEM_LIMIT),
    )(packed)


def sweep_call(packed, start_block, iters, scale):
    n, k = start_block.shape
    return pl.pallas_call(
        functools.partial(sweep_kernel, iters, scale),
        out_shape=jax.ShapeDtypeStruct((n, k), jnp.float32),
        in_specs=[pl.BlockSpec(memory_space=pltpu.VMEM)] * 2,
        out_specs=pl.BlockSpec(memory_space=pltpu.VMEM),
        scratch_shapes=[pltpu.VMEM((n, n), jnp.float32)],
        compiler_params=pltpu.CompilerParams(vmem_limit_bytes=VMEM_LIMIT),
    )(packed, start_block)


def tail_split(packed, start_block, iters, scale):
    n, k = start_block.shape
    core = lax.axis_index("dof") % 2

    def factor_side(a, b):
        return chol_call(a, n, scale), jnp.zeros((n, k), jnp.float32)

    def sweep_side(a, b):
        return jnp.zeros((n, n), jnp.float32), sweep_call(a, b, iters, scale)

    r_loc, b_loc = lax.cond(core == 0, factor_side, sweep_side, packed, start_block)
    pairs = lax.axis_size("dof") // 2
    r_in = lax.ppermute(r_loc, "dof", [(2 * i, 2 * i + 1) for i in range(pairs)])
    b_in = lax.ppermute(b_loc, "dof", [(2 * i + 1, 2 * i) for i in range(pairs)])
    return r_loc + r_in, b_loc + b_in


STEPS = 64
ITERS = 3
PASSES = 16
TILE = 128


def pack_upper(rows):
    width = rows.shape[1]
    pieces = []
    for i in range(width // TILE):
        lhs = rows[:, i * TILE:(i + 1) * TILE]
        rhs = rows[:, i * TILE:]
        pieces.append(
            lax.dot_general(lhs, rhs, (((0,), (0,)), ((), ())), preferred_element_type=jnp.float32)
        )
    return jnp.concatenate(pieces, axis=1)


def all_reduce_a2a(x, axes):
    rows, cols = x.shape
    half = rows // 2
    ndof = lax.axis_size("dof")
    nsnap = lax.axis_size("snap")
    core = lax.axis_index("dof") % 2
    swap = [(i, i ^ 1) for i in range(ndof)]
    mine = lax.dynamic_slice_in_dim(x, core * half, half, 0)
    theirs = lax.dynamic_slice_in_dim(x, (1 - core) * half, half, 0)
    own = mine + lax.ppermute(theirs, "dof", swap)
    stacked = jnp.concatenate([own[:, :cols // 2], own[:, cols // 2:]], axis=0)
    received = lax.all_to_all(stacked, axes, 0, 0, tiled=True)
    by_core = received.reshape(ndof // 2, 2, nsnap, cols // 2).sum(axis=(0, 2))
    spread = jnp.broadcast_to(by_core[None, :, None, :], (ndof // 2, 2, nsnap, cols // 2))
    gathered = lax.all_to_all(spread.reshape(rows, cols // 2), axes, 0, 0, tiled=True)
    own_total = jnp.concatenate([gathered[:half], gathered[half:]], axis=1)
    other_total = lax.ppermute(own_total, "dof", swap)
    first = jnp.where(core == 0, own_total, other_total)
    second = jnp.where(core == 0, other_total, own_total)
    return jnp.concatenate([first, second], axis=0)


def body(snapshots, lengths, start_block):
    rows = lax.all_to_all(snapshots, "snap", 0, 1, tiled=True)
    width = rows.shape[1]
    col_length = jnp.repeat(lengths, STEPS, total_repeat_length=width)
    columns = jnp.arange(width, dtype=jnp.int32)
    active = columns % STEPS < col_length
    masked = jnp.where(active[None, :], rows, jnp.zeros_like(rows))
    row_count = snapshots.shape[0] * lax.axis_size("dof")
    packed = all_reduce_a2a(pack_upper(masked), ("dof", "snap"))
    upper_factor, subspace = tail_split(packed, start_block, ITERS, 1.0 / row_count)
    hi32 = lax.reduce_precision(subspace, exponent_bits=8, mantissa_bits=7)
    rest = subspace - hi32
    mid32 = lax.reduce_precision(rest, exponent_bits=8, mantissa_bits=7)
    lo32 = lax.reduce_precision(rest - mid32, exponent_bits=8, mantissa_bits=7)
    pod_modes = sum(
        jnp.dot(masked, p.astype(jnp.bfloat16), preferred_element_type=jnp.float32)
        for p in (hi32, mid32, lo32)
    )
    return (pod_modes, upper_factor)


def solution(mesh):
    placed = (P("dof", "snap"), P(), P())
    return jax.shard_map(
        body, mesh=mesh, in_specs=placed, out_specs=(P(("dof", "snap"), None), P()), check_vma=False
    )
```

```python
import functools
import jax
import jax.numpy as jnp
from jax import lax
from jax.experimental import pallas as pl
from jax.experimental.pallas import tpu as pltpu
from jax.sharding import PartitionSpec as P


HI = lax.Precision.HIGHEST
MID = lax.Precision.HIGH
LEAF = 128


def mm(a, b, precision=HI):
    return jnp.dot(a, b, precision=precision, preferred_element_type=jnp.float32)


def mm_tn(a, b, precision=HI):
    return lax.dot_general(a, b, (((0,), (0,)), ((), ())), precision=precision, preferred_element_type=jnp.float32)


def mm_nt(a, b):
    return lax.dot_general(a, b, (((1,), (1,)), ((), ())), precision=HI, preferred_element_type=jnp.float32)


def leaf_chol_inv(a):
    n = a.shape[0]
    row = lax.broadcasted_iota(jnp.int32, (n, 2 * n), 0)
    lane = lax.broadcasted_iota(jnp.int32, (n, 2 * n), 1)
    eye = jnp.where(row == lane - n, 1.0, 0.0).astype(jnp.float32)
    m0 = jnp.where(lane < n, jnp.concatenate([a, a], axis=1), eye)
    r2 = lax.broadcasted_iota(jnp.int32, (n, n), 0)
    c2 = lax.broadcasted_iota(jnp.int32, (n, n), 1)
    d0 = jnp.sum(jnp.where(r2 == c2, a, 0.0), axis=0, keepdims=True)
    row1 = lax.broadcasted_iota(jnp.int32, (n, 1), 0)
    lane1 = lax.broadcasted_iota(jnp.int32, (1, n), 1)

    def step(j, carry):
        m, d = carry
        pivot = jnp.sum(jnp.where(lane1 == j, d, 0.0), axis=1, keepdims=True)
        s = lax.rsqrt(pivot)
        pick_row = row == j
        prow = jnp.sum(jnp.where(pick_row, m, 0.0), axis=0, keepdims=True)
        col = jnp.sum(jnp.where(lane[:, :n] == j, m[:, :n], 0.0), axis=1, keepdims=True)
        nrow = prow * s
        mult = jnp.where(row1 > j, col * s, 0.0)
        head = nrow[:, :n]
        return jnp.where(pick_row, nrow, m - mult * nrow), d - head * head

    m, _ = lax.fori_loop(0, n, step, (m0, d0), unroll=4)
    u = jnp.where(r2 <= c2, m[:, :n], 0.0)
    w = m[:, n:]
    return u, w


def chol_inv(a, need_w):
    n = a.shape[0]
    if n <= LEAF:
        return leaf_chol_inv(a)
    h = n // 2
    u11, w11 = chol_inv(a[:h, :h], True)
    u12 = mm(w11, a[:h, h:], MID)
    s = a[h:, h:] - mm_tn(u12, u12, MID)
    u22, w22 = chol_inv(s, need_w)
    u = jnp.concatenate(
        [jnp.concatenate([u11, u12], axis=1),
         jnp.concatenate([jnp.zeros((h, h), jnp.float32), u22], axis=1)], axis=0)
    if not need_w:
        return u, None
    w21 = -mm(w22, mm_tn(u12, w11, MID), MID)
    w = jnp.concatenate(
        [jnp.concatenate([w11, jnp.zeros((h, h), jnp.float32)], axis=1),
         jnp.concatenate([w21, w22], axis=1)], axis=0)
    return u, w


def build_shifted(p_ref, sref, scale):
    n = sref.shape[0]
    eye = jnp.where(lax.broadcasted_iota(jnp.int32, (TILE, TILE), 0)
                    == lax.broadcasted_iota(jnp.int32, (TILE, TILE), 1), 0.05, 0.0).astype(jnp.float32)
    offset = 0
    for i in range(n // TILE):
        for j in range(i, n // TILE):
            c0 = offset + (j - i) * TILE
            blk = p_ref[:, c0:c0 + TILE] * scale
            if i == j:
                sref[i * TILE:(i + 1) * TILE, j * TILE:(j + 1) * TILE] = blk + eye
            else:
                sref[i * TILE:(i + 1) * TILE, j * TILE:(j + 1) * TILE] = blk
                sref[j * TILE:(j + 1) * TILE, i * TILE:(i + 1) * TILE] = jnp.transpose(blk)
        offset += n - i * TILE


def chol_kernel(scale, p_ref, r_ref, sref):
    build_shifted(p_ref, sref, scale)
    u, _ = chol_inv(sref[...], False)
    r_ref[...] = u


def sweep_kernel(iters, scale, p_ref, b_ref, out_ref, sref):
    build_shifted(p_ref, sref, scale)
    blk = b_ref[...]
    for _ in range(iters):
        image = mm(sref[...], blk)
        corr = mm_tn(image, image)
        _, w = chol_inv(corr, True)
        blk = mm_nt(image, w)
    out_ref[...] = blk


VMEM_LIMIT = 60 * 1024 * 1024


def chol_call(packed, n, scale):
    return pl.pallas_call(
        functools.partial(chol_kernel, scale),
        out_shape=jax.ShapeDtypeStruct((n, n), jnp.float32),
        in_specs=[pl.BlockSpec(memory_space=pltpu.VMEM)],
        out_specs=pl.BlockSpec(memory_space=pltpu.VMEM),
        scratch_shapes=[pltpu.VMEM((n, n), jnp.float32)],
        compiler_params=pltpu.CompilerParams(vmem_limit_bytes=VMEM_LIMIT),
    )(packed)


def sweep_call(packed, start_block, iters, scale):
    n, k = start_block.shape
    return pl.pallas_call(
        functools.partial(sweep_kernel, iters, scale),
        out_shape=jax.ShapeDtypeStruct((n, k), jnp.float32),
        in_specs=[pl.BlockSpec(memory_space=pltpu.VMEM)] * 2,
        out_specs=pl.BlockSpec(memory_space=pltpu.VMEM),
        scratch_shapes=[pltpu.VMEM((n, n), jnp.float32)],
        compiler_params=pltpu.CompilerParams(vmem_limit_bytes=VMEM_LIMIT),
    )(packed, start_block)


def tail_split(packed, start_block, iters, scale):
    n, k = start_block.shape
    core = lax.axis_index("dof") % 2

    def factor_side(a, b):
        return chol_call(a, n, scale), jnp.zeros((n, k), jnp.float32)

    def sweep_side(a, b):
        return jnp.zeros((n, n), jnp.float32), sweep_call(a, b, iters, scale)

    r_loc, b_loc = lax.cond(core == 0, factor_side, sweep_side, packed, start_block)
    pairs = lax.axis_size("dof") // 2
    r_in = lax.ppermute(r_loc, "dof", [(2 * i, 2 * i + 1) for i in range(pairs)])
    b_in = lax.ppermute(b_loc, "dof", [(2 * i + 1, 2 * i) for i in range(pairs)])
    return r_loc + r_in, b_loc + b_in


STEPS = 64
ITERS = 3
PASSES = 16
TILE = 128


def pack_upper(rows):
    width = rows.shape[1]
    pieces = []
    for i in range(width // TILE):
        lhs = rows[:, i * TILE:(i + 1) * TILE]
        rhs = rows[:, i * TILE:]
        pieces.append(
            lax.dot_general(lhs, rhs, (((0,), (0,)), ((), ())), preferred_element_type=jnp.float32)
        )
    return jnp.concatenate(pieces, axis=1)


def all_reduce_a2a(x, axes):
    rows, cols = x.shape
    half = rows // 2
    ndof = lax.axis_size("dof")
    nsnap = lax.axis_size("snap")
    core = lax.axis_index("dof") % 2
    swap = [(i, i ^ 1) for i in range(ndof)]
    mine = lax.dynamic_slice_in_dim(x, core * half, half, 0)
    theirs = lax.dynamic_slice_in_dim(x, (1 - core) * half, half, 0)
    own = mine + lax.ppermute(theirs, "dof", swap)
    stacked = jnp.concatenate([own[:, :cols // 2], own[:, cols // 2:]], axis=0)
    received = lax.all_to_all(stacked, axes, 0, 0, tiled=True)
    by_core = received.reshape(ndof // 2, 2, nsnap, cols // 2).sum(axis=(0, 2))
    spread = jnp.broadcast_to(by_core[None, :, None, :], (ndof // 2, 2, nsnap, cols // 2))
    gathered = lax.all_to_all(spread.reshape(rows, cols // 2), axes, 0, 0, tiled=True)
    own_total = jnp.concatenate([gathered[:half], gathered[half:]], axis=1)
    other_total = lax.ppermute(own_total, "dof", swap)
    first = jnp.where(core == 0, own_total, other_total)
    second = jnp.where(core == 0, other_total, own_total)
    return jnp.concatenate([first, second], axis=0)


def body(snapshots, lengths, start_block):
    rows = lax.all_to_all(snapshots, "snap", 0, 1, tiled=True)
    width = rows.shape[1]
    col_length = jnp.repeat(lengths, STEPS, total_repeat_length=width)
    columns = jnp.arange(width, dtype=jnp.int32)
    active = columns % STEPS < col_length
    masked = jnp.where(active[None, :], rows, jnp.zeros_like(rows))
    row_count = snapshots.shape[0] * lax.axis_size("dof")
    packed = all_reduce_a2a(pack_upper(masked), ("dof", "snap"))
    upper_factor, subspace = tail_split(packed, start_block, ITERS, 1.0 / row_count)
    pod_modes = jnp.dot(
        masked.astype(jnp.float32), subspace, precision=lax.Precision.HIGH,
        preferred_element_type=jnp.float32,
    )
    return (pod_modes, upper_factor)


def solution(mesh):
    placed = (P("dof", "snap"), P(), P())
    return jax.shard_map(
        body, mesh=mesh, in_specs=placed, out_specs=(P(("dof", "snap"), None), P()), check_vma=False
    )
```

```python
import functools
import jax
import jax.numpy as jnp
from jax import lax
from jax.experimental import pallas as pl
from jax.experimental.pallas import tpu as pltpu
from jax.sharding import PartitionSpec as P


HI = lax.Precision.HIGHEST
MID = lax.Precision.HIGH
LEAF = 128


def mm(a, b, precision=HI):
    return jnp.dot(a, b, precision=precision, preferred_element_type=jnp.float32)


def mm_tn(a, b, precision=HI):
    return lax.dot_general(a, b, (((0,), (0,)), ((), ())), precision=precision, preferred_element_type=jnp.float32)


def mm_nt(a, b):
    return lax.dot_general(a, b, (((1,), (1,)), ((), ())), precision=HI, preferred_element_type=jnp.float32)


def leaf_chol_inv(a, unroll):
    n = a.shape[0]
    row = lax.broadcasted_iota(jnp.int32, (n, 2 * n), 0)
    lane = lax.broadcasted_iota(jnp.int32, (n, 2 * n), 1)
    eye = jnp.where(row == lane - n, 1.0, 0.0).astype(jnp.float32)
    m0 = jnp.where(lane < n, jnp.concatenate([a, a], axis=1), eye)
    r2 = lax.broadcasted_iota(jnp.int32, (n, n), 0)
    c2 = lax.broadcasted_iota(jnp.int32, (n, n), 1)
    d0 = jnp.sum(jnp.where(r2 == c2, a, 0.0), axis=0, keepdims=True)
    row1 = lax.broadcasted_iota(jnp.int32, (n, 1), 0)
    lane1 = lax.broadcasted_iota(jnp.int32, (1, n), 1)

    def step(j, carry):
        m, d = carry
        pivot = jnp.sum(jnp.where(lane1 == j, d, 0.0), axis=1, keepdims=True)
        s = lax.rsqrt(pivot)
        pick_row = row == j
        prow = jnp.sum(jnp.where(pick_row, m, 0.0), axis=0, keepdims=True)
        col = jnp.sum(jnp.where(lane[:, :n] == j, m[:, :n], 0.0), axis=1, keepdims=True)
        nrow = prow * s
        mult = jnp.where(row1 > j, col * s, 0.0)
        head = nrow[:, :n]
        return jnp.where(pick_row, nrow, m - mult * nrow), d - head * head

    m, _ = lax.fori_loop(0, n, step, (m0, d0), unroll=unroll)
    u = jnp.where(r2 <= c2, m[:, :n], 0.0)
    w = m[:, n:]
    return u, w


def chol_inv(a, need_w, unroll=4):
    n = a.shape[0]
    if n <= LEAF:
        return leaf_chol_inv(a, unroll)
    h = n // 2
    u11, w11 = chol_inv(a[:h, :h], True, unroll)
    u12 = mm(w11, a[:h, h:], MID)
    s = a[h:, h:] - mm_tn(u12, u12, MID)
    u22, w22 = chol_inv(s, need_w, unroll)
    u = jnp.concatenate(
        [jnp.concatenate([u11, u12], axis=1),
         jnp.concatenate([jnp.zeros((h, h), jnp.float32), u22], axis=1)], axis=0)
    if not need_w:
        return u, None
    w21 = -mm(w22, mm_tn(u12, w11, MID), MID)
    w = jnp.concatenate(
        [jnp.concatenate([w11, jnp.zeros((h, h), jnp.float32)], axis=1),
         jnp.concatenate([w21, w22], axis=1)], axis=0)
    return u, w


def build_shifted(p_ref, sref, scale):
    n = sref.shape[0]
    eye = jnp.where(lax.broadcasted_iota(jnp.int32, (TILE, TILE), 0)
                    == lax.broadcasted_iota(jnp.int32, (TILE, TILE), 1), 0.05, 0.0).astype(jnp.float32)
    offset = 0
    for i in range(n // TILE):
        for j in range(i, n // TILE):
            c0 = offset + (j - i) * TILE
            blk = p_ref[:, c0:c0 + TILE] * scale
            if i == j:
                sref[i * TILE:(i + 1) * TILE, j * TILE:(j + 1) * TILE] = blk + eye
            else:
                sref[i * TILE:(i + 1) * TILE, j * TILE:(j + 1) * TILE] = blk
                sref[j * TILE:(j + 1) * TILE, i * TILE:(i + 1) * TILE] = jnp.transpose(blk)
        offset += n - i * TILE


def chol_kernel(scale, p_ref, r_ref, sref):
    build_shifted(p_ref, sref, scale)
    u, _ = chol_inv(sref[...], False, unroll=8)
    r_ref[...] = u


def sweep_kernel(iters, scale, p_ref, b_ref, out_ref, sref):
    build_shifted(p_ref, sref, scale)
    blk = b_ref[...]
    for _ in range(iters):
        image = mm(sref[...], blk)
        corr = mm_tn(image, image)
        _, w = chol_inv(corr, True)
        blk = mm_nt(image, w)
    out_ref[...] = blk


VMEM_LIMIT = 60 * 1024 * 1024


def chol_call(packed, n, scale):
    return pl.pallas_call(
        functools.partial(chol_kernel, scale),
        out_shape=jax.ShapeDtypeStruct((n, n), jnp.float32),
        in_specs=[pl.BlockSpec(memory_space=pltpu.VMEM)],
        out_specs=pl.BlockSpec(memory_space=pltpu.VMEM),
        scratch_shapes=[pltpu.VMEM((n, n), jnp.float32)],
        compiler_params=pltpu.CompilerParams(vmem_limit_bytes=VMEM_LIMIT),
    )(packed)


def sweep_call(packed, start_block, iters, scale):
    n, k = start_block.shape
    return pl.pallas_call(
        functools.partial(sweep_kernel, iters, scale),
        out_shape=jax.ShapeDtypeStruct((n, k), jnp.float32),
        in_specs=[pl.BlockSpec(memory_space=pltpu.VMEM)] * 2,
        out_specs=pl.BlockSpec(memory_space=pltpu.VMEM),
        scratch_shapes=[pltpu.VMEM((n, n), jnp.float32)],
        compiler_params=pltpu.CompilerParams(vmem_limit_bytes=VMEM_LIMIT),
    )(packed, start_block)


def tail_split(packed, start_block, iters, scale):
    n, k = start_block.shape
    core = lax.axis_index("dof") % 2

    def factor_side(a, b):
        return chol_call(a, n, scale), jnp.zeros((n, k), jnp.float32)

    def sweep_side(a, b):
        return jnp.zeros((n, n), jnp.float32), sweep_call(a, b, iters, scale)

    r_loc, b_loc = lax.cond(core == 0, factor_side, sweep_side, packed, start_block)
    pairs = lax.axis_size("dof") // 2
    r_in = lax.ppermute(r_loc, "dof", [(2 * i, 2 * i + 1) for i in range(pairs)])
    b_in = lax.ppermute(b_loc, "dof", [(2 * i + 1, 2 * i) for i in range(pairs)])
    return r_loc + r_in, b_loc + b_in


STEPS = 64
ITERS = 3
PASSES = 16
TILE = 128


def pack_upper(rows):
    width = rows.shape[1]
    pieces = []
    for i in range(width // TILE):
        lhs = rows[:, i * TILE:(i + 1) * TILE]
        rhs = rows[:, i * TILE:]
        pieces.append(
            lax.dot_general(lhs, rhs, (((0,), (0,)), ((), ())), preferred_element_type=jnp.float32)
        )
    return jnp.concatenate(pieces, axis=1)


def all_reduce_a2a(x, axes):
    rows, cols = x.shape
    half = rows // 2
    ndof = lax.axis_size("dof")
    nsnap = lax.axis_size("snap")
    core = lax.axis_index("dof") % 2
    swap = [(i, i ^ 1) for i in range(ndof)]
    mine = lax.dynamic_slice_in_dim(x, core * half, half, 0)
    theirs = lax.dynamic_slice_in_dim(x, (1 - core) * half, half, 0)
    own = mine + lax.ppermute(theirs, "dof", swap)
    stacked = jnp.concatenate([own[:, :cols // 2], own[:, cols // 2:]], axis=0)
    received = lax.all_to_all(stacked, axes, 0, 0, tiled=True)
    by_core = received.reshape(ndof // 2, 2, nsnap, cols // 2).sum(axis=(0, 2))
    spread = jnp.broadcast_to(by_core[None, :, None, :], (ndof // 2, 2, nsnap, cols // 2))
    gathered = lax.all_to_all(spread.reshape(rows, cols // 2), axes, 0, 0, tiled=True)
    own_total = jnp.concatenate([gathered[:half], gathered[half:]], axis=1)
    other_total = lax.ppermute(own_total, "dof", swap)
    first = jnp.where(core == 0, own_total, other_total)
    second = jnp.where(core == 0, other_total, own_total)
    return jnp.concatenate([first, second], axis=0)


def body(snapshots, lengths, start_block):
    rows = lax.all_to_all(snapshots, "snap", 0, 1, tiled=True)
    width = rows.shape[1]
    col_length = jnp.repeat(lengths, STEPS, total_repeat_length=width)
    columns = jnp.arange(width, dtype=jnp.int32)
    active = columns % STEPS < col_length
    masked = jnp.where(active[None, :], rows, jnp.zeros_like(rows))
    row_count = snapshots.shape[0] * lax.axis_size("dof")
    packed = all_reduce_a2a(pack_upper(masked), ("dof", "snap"))
    upper_factor, subspace = tail_split(packed, start_block, ITERS, 1.0 / row_count)
    pod_modes = jnp.dot(
        masked.astype(jnp.float32), subspace, precision=lax.Precision.HIGH,
        preferred_element_type=jnp.float32,
    )
    return (pod_modes, upper_factor)


def solution(mesh):
    placed = (P("dof", "snap"), P(), P())
    return jax.shard_map(
        body, mesh=mesh, in_specs=placed, out_specs=(P(("dof", "snap"), None), P()), check_vma=False
    )
```

```python
import functools
import jax
import jax.numpy as jnp
from jax import lax
from jax.experimental import pallas as pl
from jax.experimental.pallas import tpu as pltpu
from jax.sharding import PartitionSpec as P


HI = lax.Precision.HIGHEST
MID = lax.Precision.HIGH
LEAF = 128


def mm(a, b, precision=HI):
    return jnp.dot(a, b, precision=precision, preferred_element_type=jnp.float32)


def mm_tn(a, b, precision=HI):
    return lax.dot_general(a, b, (((0,), (0,)), ((), ())), precision=precision, preferred_element_type=jnp.float32)


def mm_nt(a, b):
    return lax.dot_general(a, b, (((1,), (1,)), ((), ())), precision=HI, preferred_element_type=jnp.float32)


def leaf_chol_inv(a, unroll):
    n = a.shape[0]
    row = lax.broadcasted_iota(jnp.int32, (n, 2 * n), 0)
    lane = lax.broadcasted_iota(jnp.int32, (n, 2 * n), 1)
    eye = jnp.where(row == lane - n, 1.0, 0.0).astype(jnp.float32)
    m0 = jnp.where(lane < n, jnp.concatenate([a, a], axis=1), eye)
    r2 = lax.broadcasted_iota(jnp.int32, (n, n), 0)
    c2 = lax.broadcasted_iota(jnp.int32, (n, n), 1)
    d0 = jnp.sum(jnp.where(r2 == c2, a, 0.0), axis=0, keepdims=True)
    row1 = lax.broadcasted_iota(jnp.int32, (n, 1), 0)
    lane1 = lax.broadcasted_iota(jnp.int32, (1, n), 1)

    def step(j, carry):
        m, d = carry
        pivot = jnp.sum(jnp.where(lane1 == j, d, 0.0), axis=1, keepdims=True)
        s = lax.rsqrt(pivot)
        pick_row = row == j
        prow = jnp.sum(jnp.where(pick_row, m, 0.0), axis=0, keepdims=True)
        col = jnp.sum(jnp.where(lane[:, :n] == j, m[:, :n], 0.0), axis=1, keepdims=True)
        nrow = prow * s
        mult = jnp.where(row1 > j, col * s, 0.0)
        head = nrow[:, :n]
        return jnp.where(pick_row, nrow, m - mult * nrow), d - head * head

    m, _ = lax.fori_loop(0, n, step, (m0, d0), unroll=unroll)
    u = jnp.where(r2 <= c2, m[:, :n], 0.0)
    w = m[:, n:]
    return u, w


def chol_inv(a, need_w, unroll=4):
    n = a.shape[0]
    if n <= LEAF:
        return leaf_chol_inv(a, unroll)
    h = n // 2
    u11, w11 = chol_inv(a[:h, :h], True, unroll)
    u12 = mm(w11, a[:h, h:], MID)
    s = a[h:, h:] - mm_tn(u12, u12, MID)
    u22, w22 = chol_inv(s, need_w, unroll)
    u = jnp.concatenate(
        [jnp.concatenate([u11, u12], axis=1),
         jnp.concatenate([jnp.zeros((h, h), jnp.float32), u22], axis=1)], axis=0)
    if not need_w:
        return u, None
    w21 = -mm(w22, mm_tn(u12, w11, MID), MID)
    w = jnp.concatenate(
        [jnp.concatenate([w11, jnp.zeros((h, h), jnp.float32)], axis=1),
         jnp.concatenate([w21, w22], axis=1)], axis=0)
    return u, w


def build_shifted(p_ref, sref, scale):
    n = sref.shape[0]
    eye = jnp.where(lax.broadcasted_iota(jnp.int32, (TILE, TILE), 0)
                    == lax.broadcasted_iota(jnp.int32, (TILE, TILE), 1), 0.05, 0.0).astype(jnp.float32)
    offset = 0
    for i in range(n // TILE):
        for j in range(i, n // TILE):
            c0 = offset + (j - i) * TILE
            blk = p_ref[:, c0:c0 + TILE] * scale
            if i == j:
                sref[i * TILE:(i + 1) * TILE, j * TILE:(j + 1) * TILE] = blk + eye
            else:
                sref[i * TILE:(i + 1) * TILE, j * TILE:(j + 1) * TILE] = blk
                sref[j * TILE:(j + 1) * TILE, i * TILE:(i + 1) * TILE] = jnp.transpose(blk)
        offset += n - i * TILE


def chol_kernel(scale, p_ref, r_ref, sref):
    build_shifted(p_ref, sref, scale)
    u, _ = chol_inv(sref[...], False, unroll=16)
    r_ref[...] = u


def sweep_kernel(iters, scale, p_ref, b_ref, out_ref, sref):
    build_shifted(p_ref, sref, scale)
    blk = b_ref[...]
    for _ in range(iters):
        image = mm(sref[...], blk)
        corr = mm_tn(image, image)
        _, w = chol_inv(corr, True)
        blk = mm_nt(image, w)
    out_ref[...] = blk


VMEM_LIMIT = 60 * 1024 * 1024


def chol_call(packed, n, scale):
    return pl.pallas_call(
        functools.partial(chol_kernel, scale),
        out_shape=jax.ShapeDtypeStruct((n, n), jnp.float32),
        in_specs=[pl.BlockSpec(memory_space=pltpu.VMEM)],
        out_specs=pl.BlockSpec(memory_space=pltpu.VMEM),
        scratch_shapes=[pltpu.VMEM((n, n), jnp.float32)],
        compiler_params=pltpu.CompilerParams(vmem_limit_bytes=VMEM_LIMIT),
    )(packed)


def sweep_call(packed, start_block, iters, scale):
    n, k = start_block.shape
    return pl.pallas_call(
        functools.partial(sweep_kernel, iters, scale),
        out_shape=jax.ShapeDtypeStruct((n, k), jnp.float32),
        in_specs=[pl.BlockSpec(memory_space=pltpu.VMEM)] * 2,
        out_specs=pl.BlockSpec(memory_space=pltpu.VMEM),
        scratch_shapes=[pltpu.VMEM((n, n), jnp.float32)],
        compiler_params=pltpu.CompilerParams(vmem_limit_bytes=VMEM_LIMIT),
    )(packed, start_block)


def tail_split(packed, start_block, iters, scale):
    n, k = start_block.shape
    core = lax.axis_index("dof") % 2

    def factor_side(a, b):
        return chol_call(a, n, scale), jnp.zeros((n, k), jnp.float32)

    def sweep_side(a, b):
        return jnp.zeros((n, n), jnp.float32), sweep_call(a, b, iters, scale)

    r_loc, b_loc = lax.cond(core == 0, factor_side, sweep_side, packed, start_block)
    pairs = lax.axis_size("dof") // 2
    r_in = lax.ppermute(r_loc, "dof", [(2 * i, 2 * i + 1) for i in range(pairs)])
    b_in = lax.ppermute(b_loc, "dof", [(2 * i + 1, 2 * i) for i in range(pairs)])
    return r_loc + r_in, b_loc + b_in


STEPS = 64
ITERS = 3
PASSES = 16
TILE = 128


def pack_upper(rows):
    width = rows.shape[1]
    pieces = []
    for i in range(width // TILE):
        lhs = rows[:, i * TILE:(i + 1) * TILE]
        rhs = rows[:, i * TILE:]
        pieces.append(
            lax.dot_general(lhs, rhs, (((0,), (0,)), ((), ())), preferred_element_type=jnp.float32)
        )
    return jnp.concatenate(pieces, axis=1)


def all_reduce_a2a(x, axes):
    rows, cols = x.shape
    half = rows // 2
    ndof = lax.axis_size("dof")
    nsnap = lax.axis_size("snap")
    core = lax.axis_index("dof") % 2
    swap = [(i, i ^ 1) for i in range(ndof)]
    mine = lax.dynamic_slice_in_dim(x, core * half, half, 0)
    theirs = lax.dynamic_slice_in_dim(x, (1 - core) * half, half, 0)
    own = mine + lax.ppermute(theirs, "dof", swap)
    stacked = jnp.concatenate([own[:, :cols // 2], own[:, cols // 2:]], axis=0)
    received = lax.all_to_all(stacked, axes, 0, 0, tiled=True)
    by_core = received.reshape(ndof // 2, 2, nsnap, cols // 2).sum(axis=(0, 2))
    spread = jnp.broadcast_to(by_core[None, :, None, :], (ndof // 2, 2, nsnap, cols // 2))
    gathered = lax.all_to_all(spread.reshape(rows, cols // 2), axes, 0, 0, tiled=True)
    own_total = jnp.concatenate([gathered[:half], gathered[half:]], axis=1)
    other_total = lax.ppermute(own_total, "dof", swap)
    first = jnp.where(core == 0, own_total, other_total)
    second = jnp.where(core == 0, other_total, own_total)
    return jnp.concatenate([first, second], axis=0)


def body(snapshots, lengths, start_block):
    rows = lax.all_to_all(snapshots, "snap", 0, 1, tiled=True)
    width = rows.shape[1]
    col_length = jnp.repeat(lengths, STEPS, total_repeat_length=width)
    columns = jnp.arange(width, dtype=jnp.int32)
    active = columns % STEPS < col_length
    masked = jnp.where(active[None, :], rows, jnp.zeros_like(rows))
    row_count = snapshots.shape[0] * lax.axis_size("dof")
    packed = all_reduce_a2a(pack_upper(masked), ("dof", "snap"))
    upper_factor, subspace = tail_split(packed, start_block, ITERS, 1.0 / row_count)
    pod_modes = jnp.dot(
        masked.astype(jnp.float32), subspace, precision=lax.Precision.HIGH,
        preferred_element_type=jnp.float32,
    )
    return (pod_modes, upper_factor)


def solution(mesh):
    placed = (P("dof", "snap"), P(), P())
    return jax.shard_map(
        body, mesh=mesh, in_specs=placed, out_specs=(P(("dof", "snap"), None), P()), check_vma=False
    )
```

```python
import functools
import jax
import jax.numpy as jnp
from jax import lax
from jax.experimental import pallas as pl
from jax.experimental.pallas import tpu as pltpu
from jax.sharding import PartitionSpec as P


HI = lax.Precision.HIGHEST
MID = lax.Precision.HIGH
LEAF = 128


def mm(a, b, precision=HI):
    return jnp.dot(a, b, precision=precision, preferred_element_type=jnp.float32)


def mm_tn(a, b, precision=HI):
    return lax.dot_general(a, b, (((0,), (0,)), ((), ())), precision=precision, preferred_element_type=jnp.float32)


def mm_nt(a, b):
    return lax.dot_general(a, b, (((1,), (1,)), ((), ())), precision=HI, preferred_element_type=jnp.float32)


def leaf_chol_inv(a, unroll):
    n = a.shape[0]
    row = lax.broadcasted_iota(jnp.int32, (n, 2 * n), 0)
    lane = lax.broadcasted_iota(jnp.int32, (n, 2 * n), 1)
    eye = jnp.where(row == lane - n, 1.0, 0.0).astype(jnp.float32)
    m0 = jnp.where(lane < n, jnp.concatenate([a, a], axis=1), eye)
    r2 = lax.broadcasted_iota(jnp.int32, (n, n), 0)
    c2 = lax.broadcasted_iota(jnp.int32, (n, n), 1)
    d0 = jnp.sum(jnp.where(r2 == c2, a, 0.0), axis=0, keepdims=True)
    row1 = lax.broadcasted_iota(jnp.int32, (n, 1), 0)
    lane1 = lax.broadcasted_iota(jnp.int32, (1, n), 1)

    def step(j, carry):
        m, d = carry
        pivot = jnp.sum(jnp.where(lane1 == j, d, 0.0), axis=1, keepdims=True)
        s = lax.rsqrt(pivot)
        pick_row = row == j
        prow = jnp.sum(jnp.where(pick_row, m, 0.0), axis=0, keepdims=True)
        col = jnp.sum(jnp.where(lane[:, :n] == j, m[:, :n], 0.0), axis=1, keepdims=True)
        nrow = prow * s
        mult = jnp.where(row1 > j, col * s, 0.0)
        head = nrow[:, :n]
        return jnp.where(pick_row, nrow, m - mult * nrow), d - head * head

    m, _ = lax.fori_loop(0, n, step, (m0, d0), unroll=unroll)
    u = jnp.where(r2 <= c2, m[:, :n], 0.0)
    w = m[:, n:]
    return u, w


def chol_inv(a, need_w, unroll=4):
    n = a.shape[0]
    if n <= LEAF:
        return leaf_chol_inv(a, unroll)
    h = n // 2
    u11, w11 = chol_inv(a[:h, :h], True, unroll)
    u12 = mm(w11, a[:h, h:], MID)
    s = a[h:, h:] - mm_tn(u12, u12, MID)
    u22, w22 = chol_inv(s, need_w, unroll)
    u = jnp.concatenate(
        [jnp.concatenate([u11, u12], axis=1),
         jnp.concatenate([jnp.zeros((h, h), jnp.float32), u22], axis=1)], axis=0)
    if not need_w:
        return u, None
    w21 = -mm(w22, mm_tn(u12, w11, MID), MID)
    w = jnp.concatenate(
        [jnp.concatenate([w11, jnp.zeros((h, h), jnp.float32)], axis=1),
         jnp.concatenate([w21, w22], axis=1)], axis=0)
    return u, w


def build_shifted(p_ref, sref, scale):
    n = sref.shape[0]
    eye = jnp.where(lax.broadcasted_iota(jnp.int32, (TILE, TILE), 0)
                    == lax.broadcasted_iota(jnp.int32, (TILE, TILE), 1), 0.05, 0.0).astype(jnp.float32)
    offset = 0
    for i in range(n // TILE):
        for j in range(i, n // TILE):
            c0 = offset + (j - i) * TILE
            blk = p_ref[:, c0:c0 + TILE] * scale
            if i == j:
                sref[i * TILE:(i + 1) * TILE, j * TILE:(j + 1) * TILE] = blk + eye
            else:
                sref[i * TILE:(i + 1) * TILE, j * TILE:(j + 1) * TILE] = blk
                sref[j * TILE:(j + 1) * TILE, i * TILE:(i + 1) * TILE] = jnp.transpose(blk)
        offset += n - i * TILE


def chol_kernel(scale, p_ref, r_ref, sref):
    build_shifted(p_ref, sref, scale)
    u, _ = chol_inv(sref[...], False, unroll=32)
    r_ref[...] = u


def sweep_kernel(iters, scale, p_ref, b_ref, out_ref, sref):
    build_shifted(p_ref, sref, scale)
    blk = b_ref[...]
    for _ in range(iters):
        image = mm(sref[...], blk)
        corr = mm_tn(image, image)
        _, w = chol_inv(corr, True)
        blk = mm_nt(image, w)
    out_ref[...] = blk


VMEM_LIMIT = 60 * 1024 * 1024


def chol_call(packed, n, scale):
    return pl.pallas_call(
        functools.partial(chol_kernel, scale),
        out_shape=jax.ShapeDtypeStruct((n, n), jnp.float32),
        in_specs=[pl.BlockSpec(memory_space=pltpu.VMEM)],
        out_specs=pl.BlockSpec(memory_space=pltpu.VMEM),
        scratch_shapes=[pltpu.VMEM((n, n), jnp.float32)],
        compiler_params=pltpu.CompilerParams(vmem_limit_bytes=VMEM_LIMIT),
    )(packed)


def sweep_call(packed, start_block, iters, scale):
    n, k = start_block.shape
    return pl.pallas_call(
        functools.partial(sweep_kernel, iters, scale),
        out_shape=jax.ShapeDtypeStruct((n, k), jnp.float32),
        in_specs=[pl.BlockSpec(memory_space=pltpu.VMEM)] * 2,
        out_specs=pl.BlockSpec(memory_space=pltpu.VMEM),
        scratch_shapes=[pltpu.VMEM((n, n), jnp.float32)],
        compiler_params=pltpu.CompilerParams(vmem_limit_bytes=VMEM_LIMIT),
    )(packed, start_block)


def tail_split(packed, start_block, iters, scale):
    n, k = start_block.shape
    core = lax.axis_index("dof") % 2

    def factor_side(a, b):
        return chol_call(a, n, scale), jnp.zeros((n, k), jnp.float32)

    def sweep_side(a, b):
        return jnp.zeros((n, n), jnp.float32), sweep_call(a, b, iters, scale)

    r_loc, b_loc = lax.cond(core == 0, factor_side, sweep_side, packed, start_block)
    pairs = lax.axis_size("dof") // 2
    r_in = lax.ppermute(r_loc, "dof", [(2 * i, 2 * i + 1) for i in range(pairs)])
    b_in = lax.ppermute(b_loc, "dof", [(2 * i + 1, 2 * i) for i in range(pairs)])
    return r_loc + r_in, b_loc + b_in


STEPS = 64
ITERS = 3
PASSES = 16
TILE = 128


def pack_upper(rows):
    width = rows.shape[1]
    pieces = []
    for i in range(width // TILE):
        lhs = rows[:, i * TILE:(i + 1) * TILE]
        rhs = rows[:, i * TILE:]
        pieces.append(
            lax.dot_general(lhs, rhs, (((0,), (0,)), ((), ())), preferred_element_type=jnp.float32)
        )
    return jnp.concatenate(pieces, axis=1)


def all_reduce_a2a(x, axes):
    rows, cols = x.shape
    half = rows // 2
    ndof = lax.axis_size("dof")
    nsnap = lax.axis_size("snap")
    core = lax.axis_index("dof") % 2
    swap = [(i, i ^ 1) for i in range(ndof)]
    mine = lax.dynamic_slice_in_dim(x, core * half, half, 0)
    theirs = lax.dynamic_slice_in_dim(x, (1 - core) * half, half, 0)
    own = mine + lax.ppermute(theirs, "dof", swap)
    stacked = jnp.concatenate([own[:, :cols // 2], own[:, cols // 2:]], axis=0)
    received = lax.all_to_all(stacked, axes, 0, 0, tiled=True)
    by_core = received.reshape(ndof // 2, 2, nsnap, cols // 2).sum(axis=(0, 2))
    spread = jnp.broadcast_to(by_core[None, :, None, :], (ndof // 2, 2, nsnap, cols // 2))
    gathered = lax.all_to_all(spread.reshape(rows, cols // 2), axes, 0, 0, tiled=True)
    own_total = jnp.concatenate([gathered[:half], gathered[half:]], axis=1)
    other_total = lax.ppermute(own_total, "dof", swap)
    first = jnp.where(core == 0, own_total, other_total)
    second = jnp.where(core == 0, other_total, own_total)
    return jnp.concatenate([first, second], axis=0)


def body(snapshots, lengths, start_block):
    rows = lax.all_to_all(snapshots, "snap", 0, 1, tiled=True)
    width = rows.shape[1]
    col_length = jnp.repeat(lengths, STEPS, total_repeat_length=width)
    columns = jnp.arange(width, dtype=jnp.int32)
    active = columns % STEPS < col_length
    masked = jnp.where(active[None, :], rows, jnp.zeros_like(rows))
    row_count = snapshots.shape[0] * lax.axis_size("dof")
    packed = all_reduce_a2a(pack_upper(masked), ("dof", "snap"))
    upper_factor, subspace = tail_split(packed, start_block, ITERS, 1.0 / row_count)
    pod_modes = jnp.dot(
        masked.astype(jnp.float32), subspace, precision=lax.Precision.HIGH,
        preferred_element_type=jnp.float32,
    )
    return (pod_modes, upper_factor)


def solution(mesh):
    placed = (P("dof", "snap"), P(), P())
    return jax.shard_map(
        body, mesh=mesh, in_specs=placed, out_specs=(P(("dof", "snap"), None), P()), check_vma=False
    )
```

```python
import functools
import jax
import jax.numpy as jnp
from jax import lax
from jax.experimental import pallas as pl
from jax.experimental.pallas import tpu as pltpu
from jax.sharding import PartitionSpec as P


HI = lax.Precision.HIGHEST
MID = lax.Precision.HIGH
LEAF = 128


def mm(a, b, precision=HI):
    return jnp.dot(a, b, precision=precision, preferred_element_type=jnp.float32)


def mm_tn(a, b, precision=HI):
    return lax.dot_general(a, b, (((0,), (0,)), ((), ())), precision=precision, preferred_element_type=jnp.float32)


def mm_nt(a, b):
    return lax.dot_general(a, b, (((1,), (1,)), ((), ())), precision=HI, preferred_element_type=jnp.float32)


def leaf_chol_inv(a, unroll):
    n = a.shape[0]
    row = lax.broadcasted_iota(jnp.int32, (n, 2 * n), 0)
    lane = lax.broadcasted_iota(jnp.int32, (n, 2 * n), 1)
    eye = jnp.where(row == lane - n, 1.0, 0.0).astype(jnp.float32)
    m0 = jnp.where(lane < n, jnp.concatenate([a, a], axis=1), eye)
    r2 = lax.broadcasted_iota(jnp.int32, (n, n), 0)
    c2 = lax.broadcasted_iota(jnp.int32, (n, n), 1)
    d0 = jnp.sum(jnp.where(r2 == c2, a, 0.0), axis=0, keepdims=True)
    row1 = lax.broadcasted_iota(jnp.int32, (n, 1), 0)
    lane1 = lax.broadcasted_iota(jnp.int32, (1, n), 1)

    def step(j, carry):
        m, d = carry
        pivot = jnp.sum(jnp.where(lane1 == j, d, 0.0), axis=1, keepdims=True)
        s = lax.rsqrt(pivot)
        pick_row = row == j
        prow = jnp.sum(jnp.where(pick_row, m, 0.0), axis=0, keepdims=True)
        col = jnp.sum(jnp.where(lane[:, :n] == j, m[:, :n], 0.0), axis=1, keepdims=True)
        nrow = prow * s
        mult = jnp.where(row1 > j, col * s, 0.0)
        head = nrow[:, :n]
        return jnp.where(pick_row, nrow, m - mult * nrow), d - head * head

    m, _ = lax.fori_loop(0, n, step, (m0, d0), unroll=unroll)
    u = jnp.where(r2 <= c2, m[:, :n], 0.0)
    w = m[:, n:]
    return u, w


def chol_inv(a, need_w, unroll=4):
    n = a.shape[0]
    if n <= LEAF:
        return leaf_chol_inv(a, unroll)
    h = n // 2
    u11, w11 = chol_inv(a[:h, :h], True, unroll)
    u12 = mm(w11, a[:h, h:], MID)
    s = a[h:, h:] - mm_tn(u12, u12, MID)
    u22, w22 = chol_inv(s, need_w, unroll)
    u = jnp.concatenate(
        [jnp.concatenate([u11, u12], axis=1),
         jnp.concatenate([jnp.zeros((h, h), jnp.float32), u22], axis=1)], axis=0)
    if not need_w:
        return u, None
    w21 = -mm(w22, mm_tn(u12, w11, MID), MID)
    w = jnp.concatenate(
        [jnp.concatenate([w11, jnp.zeros((h, h), jnp.float32)], axis=1),
         jnp.concatenate([w21, w22], axis=1)], axis=0)
    return u, w


def build_shifted(p_ref, sref, scale):
    n = sref.shape[0]
    eye = jnp.where(lax.broadcasted_iota(jnp.int32, (TILE, TILE), 0)
                    == lax.broadcasted_iota(jnp.int32, (TILE, TILE), 1), 0.05, 0.0).astype(jnp.float32)
    offset = 0
    for i in range(n // TILE):
        for j in range(i, n // TILE):
            c0 = offset + (j - i) * TILE
            blk = p_ref[:, c0:c0 + TILE] * scale
            if i == j:
                sref[i * TILE:(i + 1) * TILE, j * TILE:(j + 1) * TILE] = blk + eye
            else:
                sref[i * TILE:(i + 1) * TILE, j * TILE:(j + 1) * TILE] = blk
                sref[j * TILE:(j + 1) * TILE, i * TILE:(i + 1) * TILE] = jnp.transpose(blk)
        offset += n - i * TILE


def chol_kernel(scale, p_ref, r_ref, sref):
    build_shifted(p_ref, sref, scale)
    u, _ = chol_inv(sref[...], False, unroll=64)
    r_ref[...] = u


def sweep_kernel(iters, scale, p_ref, b_ref, out_ref, sref):
    build_shifted(p_ref, sref, scale)
    blk = b_ref[...]
    for _ in range(iters):
        image = mm(sref[...], blk)
        corr = mm_tn(image, image)
        _, w = chol_inv(corr, True)
        blk = mm_nt(image, w)
    out_ref[...] = blk


VMEM_LIMIT = 60 * 1024 * 1024


def chol_call(packed, n, scale):
    return pl.pallas_call(
        functools.partial(chol_kernel, scale),
        out_shape=jax.ShapeDtypeStruct((n, n), jnp.float32),
        in_specs=[pl.BlockSpec(memory_space=pltpu.VMEM)],
        out_specs=pl.BlockSpec(memory_space=pltpu.VMEM),
        scratch_shapes=[pltpu.VMEM((n, n), jnp.float32)],
        compiler_params=pltpu.CompilerParams(vmem_limit_bytes=VMEM_LIMIT),
    )(packed)


def sweep_call(packed, start_block, iters, scale):
    n, k = start_block.shape
    return pl.pallas_call(
        functools.partial(sweep_kernel, iters, scale),
        out_shape=jax.ShapeDtypeStruct((n, k), jnp.float32),
        in_specs=[pl.BlockSpec(memory_space=pltpu.VMEM)] * 2,
        out_specs=pl.BlockSpec(memory_space=pltpu.VMEM),
        scratch_shapes=[pltpu.VMEM((n, n), jnp.float32)],
        compiler_params=pltpu.CompilerParams(vmem_limit_bytes=VMEM_LIMIT),
    )(packed, start_block)


def tail_split(packed, start_block, iters, scale):
    n, k = start_block.shape
    core = lax.axis_index("dof") % 2

    def factor_side(a, b):
        return chol_call(a, n, scale), jnp.zeros((n, k), jnp.float32)

    def sweep_side(a, b):
        return jnp.zeros((n, n), jnp.float32), sweep_call(a, b, iters, scale)

    r_loc, b_loc = lax.cond(core == 0, factor_side, sweep_side, packed, start_block)
    pairs = lax.axis_size("dof") // 2
    r_in = lax.ppermute(r_loc, "dof", [(2 * i, 2 * i + 1) for i in range(pairs)])
    b_in = lax.ppermute(b_loc, "dof", [(2 * i + 1, 2 * i) for i in range(pairs)])
    return r_loc + r_in, b_loc + b_in


STEPS = 64
ITERS = 3
PASSES = 16
TILE = 128


def pack_upper(rows):
    width = rows.shape[1]
    pieces = []
    for i in range(width // TILE):
        lhs = rows[:, i * TILE:(i + 1) * TILE]
        rhs = rows[:, i * TILE:]
        pieces.append(
            lax.dot_general(lhs, rhs, (((0,), (0,)), ((), ())), preferred_element_type=jnp.float32)
        )
    return jnp.concatenate(pieces, axis=1)


def all_reduce_a2a(x, axes):
    rows, cols = x.shape
    half = rows // 2
    ndof = lax.axis_size("dof")
    nsnap = lax.axis_size("snap")
    core = lax.axis_index("dof") % 2
    swap = [(i, i ^ 1) for i in range(ndof)]
    mine = lax.dynamic_slice_in_dim(x, core * half, half, 0)
    theirs = lax.dynamic_slice_in_dim(x, (1 - core) * half, half, 0)
    own = mine + lax.ppermute(theirs, "dof", swap)
    stacked = jnp.concatenate([own[:, :cols // 2], own[:, cols // 2:]], axis=0)
    received = lax.all_to_all(stacked, axes, 0, 0, tiled=True)
    by_core = received.reshape(ndof // 2, 2, nsnap, cols // 2).sum(axis=(0, 2))
    spread = jnp.broadcast_to(by_core[None, :, None, :], (ndof // 2, 2, nsnap, cols // 2))
    gathered = lax.all_to_all(spread.reshape(rows, cols // 2), axes, 0, 0, tiled=True)
    own_total = jnp.concatenate([gathered[:half], gathered[half:]], axis=1)
    other_total = lax.ppermute(own_total, "dof", swap)
    first = jnp.where(core == 0, own_total, other_total)
    second = jnp.where(core == 0, other_total, own_total)
    return jnp.concatenate([first, second], axis=0)


def body(snapshots, lengths, start_block):
    rows = lax.all_to_all(snapshots, "snap", 0, 1, tiled=True)
    width = rows.shape[1]
    col_length = jnp.repeat(lengths, STEPS, total_repeat_length=width)
    columns = jnp.arange(width, dtype=jnp.int32)
    active = columns % STEPS < col_length
    masked = jnp.where(active[None, :], rows, jnp.zeros_like(rows))
    row_count = snapshots.shape[0] * lax.axis_size("dof")
    packed = all_reduce_a2a(pack_upper(masked), ("dof", "snap"))
    upper_factor, subspace = tail_split(packed, start_block, ITERS, 1.0 / row_count)
    pod_modes = jnp.dot(
        masked.astype(jnp.float32), subspace, precision=lax.Precision.HIGH,
        preferred_element_type=jnp.float32,
    )
    return (pod_modes, upper_factor)


def solution(mesh):
    placed = (P("dof", "snap"), P(), P())
    return jax.shard_map(
        body, mesh=mesh, in_specs=placed, out_specs=(P(("dof", "snap"), None), P()), check_vma=False
    )
```
